128 devices in a mesh: row: 8 (over z, core), col: 16 (over y, x).
Axes of the slice: x: 4, y: 4, z: 4, core: 2. Of those that a mesh axis runs over, the one named last changes fastest.
Arguments:
- state: bfloat16 [13, 1024, 4096], P(None, 'row', 'col'), may hold values from -6 to 6
- tile_ids: int32 [8, 32], P('row'), may hold values from 0 to 127, as said below
- kernel_one: bfloat16 [64, 13, 3, 3], replicated, may hold values from -0.5 to 0.5
- bias_one: float32 [64], replicated, may hold values from -3 to 3
- kernel_two: bfloat16 [64, 64, 3, 3], replicated, may hold values from -0.25 to 0.25
- bias_two: float32 [64], replicated, may hold values from -3 to 3
- kernel_three: bfloat16 [64, 64, 3, 3], replicated, may hold values from -0.25 to 0.25
- bias_three: float32 [64], replicated, may hold values from -3 to 3
- kernel_flux: bfloat16 [26, 64, 3, 3], replicated, may hold values from -0.25 to 0.25
- bias_flux: float32 [26], replicated, may hold values from -3 to 3
Outputs:
- closure: bfloat16 [13, 1024, 4096], P(None, 'row', 'col')
The draws below stay inside these ranges and needn't reach their ends.
Inputs may be any that keep to these rules, and one draw needn't show every extreme that they name: Each row of tile_ids holds 32 distinct ids in ascending order; at most 4 of them name tiles of one block, and in every row some block holds exactly that many.
All inputs are finite; a program needn't handle non-finite values.
Results may differ from the reference program's by a relative error of at most 0.012.
The reference program's roundings to bfloat16 on the way count: a program that leaves them out, or rounds other values in their place, can miss the bound.
Values may be sent and summed in bfloat16 or wider, within the bound.
No kernel may reach another device: no remote copies, remote signals or barrier semaphores. Data moves between devices by JAX's collectives and lax.ppermute only.
A program may use at most 64 MiB of HBM per device.

```python
import jax
import jax.numpy as jnp
from jax import lax

MOM = 13
HID = 64
TILE = 64
TPR = 2
TPC = 4
EVAL_TILES = 2
GH = 1024
GW = 4096
N_ROW = 8
N_COL = 16


def draw_tile_ids(key, part):
    per_block = TPR * TPC
    per_eval = EVAL_TILES
    strip_keys = jax.random.split(jax.random.fold_in(key, 17), N_ROW)

    def one_strip(strip_key):
        sub_keys = jax.random.split(strip_key, 3)
        shuffle_order = jax.random.permutation(sub_keys[0], N_COL)
        swings = jax.random.randint(sub_keys[1], (N_COL // 2,), 0, per_eval + 1)
        swings = swings.at[0].set(per_eval)
        counts = jnp.zeros((N_COL,), jnp.int32)
        counts = counts.at[shuffle_order[0::2]].set(per_eval + swings)
        counts = counts.at[shuffle_order[1::2]].set(per_eval - swings)
        owner_keys = jax.random.split(sub_keys[2], N_COL)

        def one_owner(owner_key, owner_count):
            shuffled = jax.random.permutation(owner_key, per_block)
            rank_ids = jnp.arange(per_block, dtype=jnp.int32)
            return jnp.zeros((per_block,), jnp.int32).at[shuffled].set((rank_ids < owner_count).astype(jnp.int32))
        chosen = jax.vmap(one_owner)(owner_keys, counts)
        all_ids = jnp.arange(N_COL * per_block, dtype=jnp.int32).reshape(N_COL, per_block)
        scores = jnp.where(chosen > 0, all_ids, N_COL * per_block + all_ids)
        return jnp.sort(scores.reshape(-1))[:per_eval * N_COL]
    return jax.vmap(one_strip)(strip_keys).astype(jnp.int32)


def level_of(rng, shape, pieces, smallest, largest):
    def one(axis_at, parts):
        steps = jax.random.uniform(jax.random.fold_in(jax.random.fold_in(rng, 6), axis_at), (parts,), jnp.float32, smallest / len(pieces), largest / len(pieces))
        return jnp.repeat(jnp.exp(steps), shape[axis_at] // parts).reshape((-1,) + (1,) * (len(shape) - axis_at - 1))

    loudness = one(*pieces[0])
    for cut in pieces[1:]:
        loudness = loudness * one(*cut)
    return loudness


def bell_draw(stream_key, dims, width, bound, shards=(), kind=jnp.bfloat16):
    array = width * jax.random.normal(stream_key, dims, jnp.float32)
    if shards:
        array = array * level_of(stream_key, dims, shards, -0.22, 0.18)
    return jnp.clip(array, -bound, bound).astype(kind)


def setup_inputs(seed: int = 0) -> dict:
    splits = jax.random.split(jax.random.key(seed), 11)
    return {
        "state": bell_draw(splits[0], (MOM, GH, GW), 1.0, 6.0, ((1, 8), (2, 16))),
        "tile_ids": draw_tile_ids(jax.random.fold_in(splits[10], 71), 0),
        "kernel_one": bell_draw(splits[2], (HID, MOM, 3, 3), (9 * MOM) ** -0.5, 0.5),
        "bias_one": bell_draw(splits[3], (HID,), 0.5, 3.0, (), jnp.float32),
        "kernel_two": bell_draw(splits[4], (HID, HID, 3, 3), (9 * HID) ** -0.5, 0.25),
        "bias_two": bell_draw(splits[5], (HID,), 0.5, 3.0, (), jnp.float32),
        "kernel_three": bell_draw(splits[6], (HID, HID, 3, 3), (9 * HID) ** -0.5, 0.25),
        "bias_three": bell_draw(splits[7], (HID,), 0.5, 3.0, (), jnp.float32),
        "kernel_flux": bell_draw(splits[8], (2 * MOM, HID, 3, 3), (9 * HID) ** -0.5, 0.25),
        "bias_flux": bell_draw(splits[9], (2 * MOM,), 0.5, 3.0, (), jnp.float32),
    }


dilations = (1, 2, 4, 8)


def convolve(values, kernel, bias_term, spread):
    summed = lax.conv_general_dilated(values, kernel.astype(jnp.float32), (1, 1), "VALID", rhs_dilation=(spread, spread), dimension_numbers=("NCHW", "OIHW", "NCHW"), precision=lax.Precision.HIGHEST)
    return summed + bias_term.astype(jnp.float32)[None, :, None, None]


def network(window_cells, anchor_y, anchor_x, layers, grid_h, grid_w):
    values = window_cells.astype(jnp.float32)[None]
    offset = sum(dilations)
    for layer_index in range(4):
        spread = dilations[layer_index]
        kernel, bias_term = layers[layer_index]
        summed = convolve(values, kernel, bias_term, spread)
        offset = offset - spread
        if layer_index < 3:
            indices = jnp.arange(summed.shape[2], dtype=jnp.int32)
            row_ids = anchor_y - offset + indices
            col_ids = anchor_x - offset + indices
            inside = ((row_ids >= 0) & (row_ids < grid_h))[:, None] & ((col_ids >= 0) & (col_ids < grid_w))[None, :]
            active = jnp.where(inside[None, None], jax.nn.silu(summed), 0.0)
            values = active.astype(jnp.bfloat16).astype(jnp.float32)
        else:
            values = summed
    return values[0].astype(jnp.bfloat16)


def reference(state, tile_ids, kernel_one, bias_one, kernel_two, bias_two, kernel_three, bias_three, kernel_flux, bias_flux):
    moments, grid_h, grid_w = state.shape
    margin = sum(dilations)
    per_block = TPR * TPC
    window = TILE + 2 * margin
    layers = ((kernel_one, bias_one), (kernel_two, bias_two), (kernel_three, bias_three), (kernel_flux, bias_flux))
    padded = jnp.pad(state, ((0, 0), (margin, margin), (margin, margin)))
    strips = jnp.arange(N_ROW, dtype=jnp.int32)[:, None]
    local_ids = tile_ids % per_block
    anchor_y = (strips * (TPR * TILE) + (local_ids // TPC) * TILE).reshape(-1).astype(jnp.int32)
    anchor_x = ((tile_ids // per_block) * (TPC * TILE) + (local_ids % TPC) * TILE).reshape(-1).astype(jnp.int32)

    def one_tile(anchor):
        top_cell, left_cell = anchor
        window_cells = lax.dynamic_slice(padded, (jnp.int32(0), top_cell, left_cell), (moments, window, window))
        return network(window_cells, top_cell, left_cell, layers, grid_h, grid_w)

    tile_out = lax.map(one_tile, (anchor_y, anchor_x))

    def place(position, flux_field):
        return lax.dynamic_update_slice(flux_field, tile_out[position], (jnp.int32(0), anchor_y[position], anchor_x[position]))

    flux_field = lax.fori_loop(0, anchor_y.shape[0], place, jnp.zeros((2 * moments, grid_h, grid_w), jnp.bfloat16))
    rimmed = jnp.pad(flux_field, ((0, 0), (1, 1), (1, 1)))

    def one_moment(position):
        across = lax.dynamic_index_in_dim(rimmed, position, 0, keepdims=False).astype(jnp.float32)
        downward = lax.dynamic_index_in_dim(rimmed, position + moments, 0, keepdims=False).astype(jnp.float32)
        difference = (across[1:-1, 2:] - across[1:-1, :-2]) + (downward[2:, 1:-1] - downward[:-2, 1:-1])
        return (-0.5 * difference).astype(jnp.bfloat16)

    return lax.map(one_moment, jnp.arange(moments, dtype=jnp.int32))
```

```python
import jax
import jax.numpy as jnp
from jax import lax
from jax.sharding import PartitionSpec as P

TILE = 64


dilations = (1, 2, 4, 8)


def with_halo(cells, sides, width):
    for axis, dim in sides:
        count = lax.axis_size(axis)
        ends = count - 1
        head = lax.slice_in_dim(cells, 0, width, axis=dim)
        tail = lax.slice_in_dim(cells, cells.shape[dim] - width, cells.shape[dim], axis=dim)
        cells = jnp.concatenate(
            [
                lax.ppermute(tail, axis, [(i, (i + 1) % count) for i in range(ends)]),
                cells,
                lax.ppermute(head, axis, [((i + 1) % count, i) for i in range(ends)]),
            ],
            axis=dim,
        )
    return cells


def body(
    state,
    tile_ids,
    kernel_one,
    bias_one,
    kernel_two,
    bias_two,
    kernel_three,
    bias_three,
    kernel_flux,
    bias_flux,
):
    moments, block_h, block_w = state.shape
    col_count = lax.axis_size("col")
    row_count = lax.axis_size("row")
    my_row = lax.axis_index("row")
    my_col = lax.axis_index("col")
    margin = sum(dilations)
    per_row = block_h // TILE
    per_col = block_w // TILE
    per_block = per_row * per_col
    grid_h = block_h * row_count
    grid_w = block_w * col_count
    layers = (
        (kernel_one, bias_one),
        (kernel_two, bias_two),
        (kernel_three, bias_three),
        (kernel_flux, bias_flux),
    )
    values = with_halo(state, (("row", 1), ("col", 2)), margin)[None]
    offset = margin
    for layer_index in range(4):
        spread = dilations[layer_index]
        kernel, bias_term = layers[layer_index]
        summed = lax.conv_general_dilated(
            values,
            kernel,
            (1, 1),
            "VALID",
            rhs_dilation=(spread, spread),
            dimension_numbers=("NCHW", "OIHW", "NCHW"),
            preferred_element_type=jnp.float32,
        )
        summed = summed + bias_term[None, :, None, None]
        offset = offset - spread
        if layer_index < 3:
            row_ids = my_row * block_h - offset + jnp.arange(summed.shape[2], dtype=jnp.int32)
            col_ids = my_col * block_w - offset + jnp.arange(summed.shape[3], dtype=jnp.int32)
            inside = ((row_ids >= 0) & (row_ids < grid_h))[:, None] & (
                (col_ids >= 0) & (col_ids < grid_w)
            )[None, :]
            values = jnp.where(inside[None, None], jax.nn.silu(summed), 0.0).astype(jnp.bfloat16)
        else:
            flux = summed[0]
    listed = tile_ids[0]
    mine = (listed // per_block) == my_col
    local_ids = listed % per_block
    chosen = jnp.any(
        mine[None, :] & (local_ids[None, :] == jnp.arange(per_block, dtype=jnp.int32)[:, None]), axis=1
    )
    cell_mask = jnp.broadcast_to(
        chosen.reshape(per_row, 1, per_col, 1), (per_row, TILE, per_col, TILE)
    ).reshape(block_h, block_w)
    flux_field = jnp.where(cell_mask[None], flux, 0.0).astype(jnp.bfloat16)
    rimmed = with_halo(flux_field, (("row", 1), ("col", 2)), 1)
    across = rimmed[:moments, 1:-1, :].astype(jnp.float32)
    downward = rimmed[moments:, :, 1:-1].astype(jnp.float32)
    difference = across[:, :, 2:] - across[:, :, :-2] + (downward[:, 2:, :] - downward[:, :-2, :])
    return (-0.5 * difference).astype(jnp.bfloat16)


def solution(mesh):
    return jax.shard_map(
        body,
        mesh=mesh,
        in_specs=(P(None, "row", "col"), P("row", None), P(), P(), P(), P(), P(), P(), P(), P()),
        out_specs=P(None, "row", "col"),
        check_vma=False,
    )
```

```python
import jax
import jax.numpy as jnp
from jax import lax
from jax.experimental import pallas as pl
from jax.experimental.pallas import tpu as pltpu
from jax.sharding import PartitionSpec as P

TILE = 64


dilations = (1, 2, 4, 8)
LANES = 384


def _net_kernel(lim_ref, x_ref, k1, b1, k2, b2, k3, b3, kf, bfl, out_ref, buf_a, buf_b):
    lanes = lax.broadcasted_iota(jnp.int32, (1, LANES), 1)

    def layer(src, dst, n_rows, spread, kmat, bias, index, last):
        kv = kmat[...]
        bv = bias[...]
        if not last:
            row_lo = lim_ref[4 * index]
            row_hi = lim_ref[4 * index + 1]
            col_ok = (lanes >= lim_ref[4 * index + 2]) & (lanes < lim_ref[4 * index + 3])

        def row(y, carry):
            pieces = []
            for a in range(3):
                line = src[y + spread * a]
                for e in range(3):
                    pieces.append(line if e == 0 else pltpu.roll(line, LANES - spread * e, 1))
            col = jnp.concatenate(pieces, axis=0)
            acc = jnp.dot(kv, col, preferred_element_type=jnp.float32) + bv
            if last:
                dst[y] = acc[:, : dst.shape[2]].astype(dst.dtype)
            else:
                act = acc / (1.0 + jnp.exp(-acc))
                keep = col_ok & (y >= row_lo) & (y < row_hi)
                dst[y] = jnp.where(keep, act, 0.0).astype(dst.dtype)
            return carry

        lax.fori_loop(0, n_rows, row, 0)

    h0 = x_ref.shape[0]
    h1 = h0 - 2
    h2 = h1 - 4
    h3 = h2 - 8
    h4 = h3 - 16
    layer(x_ref, buf_a, h1, 1, k1, b1, 0, False)
    layer(buf_a, buf_b, h2, 2, k2, b2, 1, False)
    layer(buf_b, buf_a, h3, 4, k3, b3, 2, False)
    layer(buf_a, out_ref, h4, 8, kf, bfl, 3, True)


def _kmat(kernel, cin):
    o, c = kernel.shape[:2]
    k = jnp.pad(kernel, ((0, 0), (0, cin - c), (0, 0), (0, 0)))
    return k.transpose(0, 2, 3, 1).reshape(o, 9 * cin)


def run_net(x, lims, layers, out_w, out_ch):
    (k1, b1), (k2, b2), (k3, b3), (kf, bf) = layers
    hid = k1.shape[0]
    h0 = x.shape[0]
    kf_p = jnp.pad(kf, ((0, out_ch - kf.shape[0]), (0, 0), (0, 0), (0, 0)))
    bf_p = jnp.pad(bf, (0, out_ch - bf.shape[0]))
    args = (
        lims, x,
        _kmat(k1, x.shape[1]), b1.reshape(-1, 1),
        _kmat(k2, hid), b2.reshape(-1, 1),
        _kmat(k3, hid), b3.reshape(-1, 1),
        _kmat(kf_p, hid), bf_p.reshape(-1, 1),
    )
    vspec = pl.BlockSpec(memory_space=pltpu.VMEM)
    return pl.pallas_call(
        _net_kernel,
        out_shape=jax.ShapeDtypeStruct((h0 - 30, out_ch, out_w), jnp.bfloat16),
        in_specs=[pl.BlockSpec(memory_space=pltpu.SMEM)] + [vspec] * 9,
        out_specs=vspec,
        scratch_shapes=[
            pltpu.VMEM((h0 - 2, hid, LANES), jnp.bfloat16),
            pltpu.VMEM((h0 - 6, hid, LANES), jnp.bfloat16),
        ],
        compiler_params=pltpu.CompilerParams(vmem_limit_bytes=56 * 1024 * 1024),
    )(*args)


def with_halo(cells, sides, width):
    for axis, dim in sides:
        count = lax.axis_size(axis)
        ends = count - 1
        head = lax.slice_in_dim(cells, 0, width, axis=dim)
        tail = lax.slice_in_dim(cells, cells.shape[dim] - width, cells.shape[dim], axis=dim)
        cells = jnp.concatenate(
            [
                lax.ppermute(tail, axis, [(i, (i + 1) % count) for i in range(ends)]),
                cells,
                lax.ppermute(head, axis, [((i + 1) % count, i) for i in range(ends)]),
            ],
            axis=dim,
        )
    return cells


def body(
    state,
    tile_ids,
    kernel_one,
    bias_one,
    kernel_two,
    bias_two,
    kernel_three,
    bias_three,
    kernel_flux,
    bias_flux,
):
    moments, block_h, block_w = state.shape
    col_count = lax.axis_size("col")
    row_count = lax.axis_size("row")
    my_row = lax.axis_index("row")
    my_col = lax.axis_index("col")
    margin = sum(dilations)
    per_row = block_h // TILE
    per_col = block_w // TILE
    per_block = per_row * per_col
    grid_h = block_h * row_count
    grid_w = block_w * col_count
    layers = (
        (kernel_one, bias_one),
        (kernel_two, bias_two),
        (kernel_three, bias_three),
        (kernel_flux, bias_flux),
    )
    extended = with_halo(state, (("row", 1), ("col", 2)), margin)
    ext_h, ext_w = extended.shape[1:]
    x = jnp.pad(extended.transpose(1, 0, 2), ((0, 0), (0, 16 - moments), (0, LANES - ext_w)))
    lims = []
    offset = margin
    out_h, out_w = ext_h, ext_w
    for spread in dilations:
        offset = offset - spread
        out_h, out_w = out_h - 2 * spread, out_w - 2 * spread
        top = offset - my_row * block_h
        left = offset - my_col * block_w
        lims += [
            jnp.maximum(top, 0),
            jnp.minimum(out_h, grid_h + top),
            jnp.maximum(left, 0),
            jnp.minimum(out_w, grid_w + left),
        ]
    lims = jnp.stack(lims).astype(jnp.int32)
    flux = run_net(x, lims, layers, block_w, 32)[:, : 2 * moments].transpose(1, 0, 2)
    listed = tile_ids[0]
    mine = (listed // per_block) == my_col
    local_ids = listed % per_block
    chosen = jnp.any(
        mine[None, :] & (local_ids[None, :] == jnp.arange(per_block, dtype=jnp.int32)[:, None]), axis=1
    )
    cell_mask = jnp.broadcast_to(
        chosen.reshape(per_row, 1, per_col, 1), (per_row, TILE, per_col, TILE)
    ).reshape(block_h, block_w)
    flux_field = jnp.where(cell_mask[None], flux, jnp.zeros((), jnp.bfloat16))
    rimmed = with_halo(flux_field, (("row", 1), ("col", 2)), 1)
    across = rimmed[:moments, 1:-1, :].astype(jnp.float32)
    downward = rimmed[moments:, :, 1:-1].astype(jnp.float32)
    difference = across[:, :, 2:] - across[:, :, :-2] + (downward[:, 2:, :] - downward[:, :-2, :])
    return (-0.5 * difference).astype(jnp.bfloat16)


def solution(mesh):
    return jax.shard_map(
        body,
        mesh=mesh,
        in_specs=(P(None, "row", "col"), P("row", None), P(), P(), P(), P(), P(), P(), P(), P()),
        out_specs=P(None, "row", "col"),
        check_vma=False,
    )
```

```python
import jax
import jax.numpy as jnp
from jax import lax
from jax.experimental import pallas as pl
from jax.experimental.pallas import tpu as pltpu
from jax.sharding import PartitionSpec as P

TILE = 64


dilations = (1, 2, 4, 8)
LANES = 384


def _net_kernel(lim_ref, x_ref, k1, b1, k2, b2, k3, b3, kf, bfl, out_ref, buf_a, buf_b):
    lanes = lax.broadcasted_iota(jnp.int32, (1, LANES), 1)

    def layer(src, dst, n_rows, spread, kmat, bias, index, last):
        kv = kmat[...]
        bv = bias[...]
        if not last:
            after = dilations[index + 1]
            row_lo = lim_ref[4 * index]
            row_hi = lim_ref[4 * index + 1]
            col_ok = (lanes >= lim_ref[4 * index + 2]) & (lanes < lim_ref[4 * index + 3])

        def row(y, carry):
            pieces = []
            for a in range(3):
                line = src[y + spread * a]
                if index == 0:
                    for e in range(3):
                        pieces.append(line if e == 0 else pltpu.roll(line, LANES - spread * e, 1))
                else:
                    pieces.append(line)
            col = jnp.concatenate(pieces, axis=0)
            acc = jnp.dot(kv, col, preferred_element_type=jnp.float32) + bv
            if last:
                dst[y] = acc[:, : dst.shape[2]].astype(dst.dtype)
            else:
                half = 0.5 * acc
                act = half + half * jnp.tanh(half)
                keep = col_ok & (y >= row_lo) & (y < row_hi)
                kept = jnp.where(keep, act, 0.0).astype(dst.dtype)
                dst[y] = jnp.concatenate(
                    [kept] + [pltpu.roll(kept, LANES - after * e, 1) for e in (1, 2)], axis=0
                )
            return carry

        lax.fori_loop(0, n_rows, row, 0, unroll=2)

    h0 = x_ref.shape[0]
    h1 = h0 - 2
    h2 = h1 - 4
    h3 = h2 - 8
    h4 = h3 - 16
    layer(x_ref, buf_a, h1, 1, k1, b1, 0, False)
    layer(buf_a, buf_b, h2, 2, k2, b2, 1, False)
    layer(buf_b, buf_a, h3, 4, k3, b3, 2, False)
    layer(buf_a, out_ref, h4, 8, kf, bfl, 3, True)


def _kmat(kernel, cin):
    o, c = kernel.shape[:2]
    k = jnp.pad(kernel, ((0, 0), (0, cin - c), (0, 0), (0, 0)))
    return k.transpose(0, 2, 3, 1).reshape(o, 9 * cin)


def run_net(x, lims, layers, out_w, out_ch):
    (k1, b1), (k2, b2), (k3, b3), (kf, bf) = layers
    hid = k1.shape[0]
    h0 = x.shape[0]
    kf_p = jnp.pad(kf, ((0, out_ch - kf.shape[0]), (0, 0), (0, 0), (0, 0)))
    bf_p = jnp.pad(bf, (0, out_ch - bf.shape[0]))
    args = (
        lims, x,
        _kmat(k1, x.shape[1]), b1.reshape(-1, 1),
        _kmat(k2, hid), b2.reshape(-1, 1),
        _kmat(k3, hid), b3.reshape(-1, 1),
        _kmat(kf_p, hid), bf_p.reshape(-1, 1),
    )
    vspec = pl.BlockSpec(memory_space=pltpu.VMEM)
    return pl.pallas_call(
        _net_kernel,
        out_shape=jax.ShapeDtypeStruct((h0 - 30, out_ch, out_w), jnp.bfloat16),
        in_specs=[pl.BlockSpec(memory_space=pltpu.SMEM)] + [vspec] * 9,
        out_specs=vspec,
        scratch_shapes=[
            pltpu.VMEM((h0 - 2, 3 * hid, LANES), jnp.bfloat16),
            pltpu.VMEM((h0 - 6, 3 * hid, LANES), jnp.bfloat16),
        ],
        compiler_params=pltpu.CompilerParams(vmem_limit_bytes=60 * 1024 * 1024),
    )(*args)


def with_halo(cells, sides, width):
    for axis, dim in sides:
        count = lax.axis_size(axis)
        ends = count - 1
        head = lax.slice_in_dim(cells, 0, width, axis=dim)
        tail = lax.slice_in_dim(cells, cells.shape[dim] - width, cells.shape[dim], axis=dim)
        cells = jnp.concatenate(
            [
                lax.ppermute(tail, axis, [(i, (i + 1) % count) for i in range(ends)]),
                cells,
                lax.ppermute(head, axis, [((i + 1) % count, i) for i in range(ends)]),
            ],
            axis=dim,
        )
    return cells


def body(
    state,
    tile_ids,
    kernel_one,
    bias_one,
    kernel_two,
    bias_two,
    kernel_three,
    bias_three,
    kernel_flux,
    bias_flux,
):
    moments, block_h, block_w = state.shape
    col_count = lax.axis_size("col")
    row_count = lax.axis_size("row")
    my_row = lax.axis_index("row")
    my_col = lax.axis_index("col")
    margin = sum(dilations)
    per_row = block_h // TILE
    per_col = block_w // TILE
    per_block = per_row * per_col
    grid_h = block_h * row_count
    grid_w = block_w * col_count
    layers = (
        (kernel_one, bias_one),
        (kernel_two, bias_two),
        (kernel_three, bias_three),
        (kernel_flux, bias_flux),
    )
    extended = with_halo(state, (("row", 1), ("col", 2)), margin)
    ext_h, ext_w = extended.shape[1:]
    x = jnp.pad(extended.transpose(1, 0, 2), ((0, 0), (0, 16 - moments), (0, LANES - ext_w)))
    lims = []
    offset = margin
    out_h, out_w = ext_h, ext_w
    for spread in dilations:
        offset = offset - spread
        out_h, out_w = out_h - 2 * spread, out_w - 2 * spread
        top = offset - my_row * block_h
        left = offset - my_col * block_w
        lims += [
            jnp.maximum(top, 0),
            jnp.minimum(out_h, grid_h + top),
            jnp.maximum(left, 0),
            jnp.minimum(out_w, grid_w + left),
        ]
    lims = jnp.stack(lims).astype(jnp.int32)
    flux = run_net(x, lims, layers, block_w, 32)[:, : 2 * moments].transpose(1, 0, 2)
    listed = tile_ids[0]
    mine = (listed // per_block) == my_col
    local_ids = listed % per_block
    chosen = jnp.any(
        mine[None, :] & (local_ids[None, :] == jnp.arange(per_block, dtype=jnp.int32)[:, None]), axis=1
    )
    cell_mask = jnp.broadcast_to(
        chosen.reshape(per_row, 1, per_col, 1), (per_row, TILE, per_col, TILE)
    ).reshape(block_h, block_w)
    flux_field = jnp.where(cell_mask[None], flux, jnp.zeros((), jnp.bfloat16))
    rimmed = with_halo(flux_field, (("row", 1), ("col", 2)), 1)
    across = rimmed[:moments, 1:-1, :].astype(jnp.float32)
    downward = rimmed[moments:, :, 1:-1].astype(jnp.float32)
    difference = across[:, :, 2:] - across[:, :, :-2] + (downward[:, 2:, :] - downward[:, :-2, :])
    return (-0.5 * difference).astype(jnp.bfloat16)


def solution(mesh):
    return jax.shard_map(
        body,
        mesh=mesh,
        in_specs=(P(None, "row", "col"), P("row", None), P(), P(), P(), P(), P(), P(), P(), P()),
        out_specs=P(None, "row", "col"),
        check_vma=False,
    )
```

```python
import jax
import jax.numpy as jnp
from jax import lax
from jax.experimental import pallas as pl
from jax.experimental.pallas import tpu as pltpu
from jax.sharding import PartitionSpec as P

TILE = 64


dilations = (1, 2, 4, 8)
LANES = 384


def _net_kernel(lim_ref, x_ref, k1, b1, k2, b2, k3, b3, kf, bfl, out_ref, buf_a, buf_b):
    lanes = lax.broadcasted_iota(jnp.int32, (1, LANES), 1)

    def layer(src, dst, n_rows, spread, kmat, bias, index, last):
        kv = kmat[...]
        bv = bias[...]
        if not last:
            after = dilations[index + 1]
            row_lo = lim_ref[4 * index]
            row_hi = lim_ref[4 * index + 1]
            col_ok = (lanes >= lim_ref[4 * index + 2]) & (lanes < lim_ref[4 * index + 3])

        def row(y, carry):
            pieces = []
            for a in range(3):
                line = src[y + spread * a]
                if index == 0:
                    for e in range(3):
                        pieces.append(line if e == 0 else pltpu.roll(line, LANES - spread * e, 1))
                else:
                    pieces.append(line)
            col = jnp.concatenate(pieces, axis=0)
            acc = jnp.dot(kv, col, preferred_element_type=jnp.float32) + bv
            if last:
                dst[y] = acc[:, : dst.shape[2]].astype(dst.dtype)
            else:
                half = 0.5 * acc
                act = half + half * jnp.tanh(half)
                keep = col_ok & (y >= row_lo) & (y < row_hi)
                kept = jnp.where(keep, act, 0.0).astype(dst.dtype)
                dst[y] = jnp.concatenate(
                    [kept] + [pltpu.roll(kept, LANES - after * e, 1) for e in (1, 2)], axis=0
                )
            return carry

        lax.fori_loop(0, n_rows, row, 0, unroll=2)

    h0 = x_ref.shape[0]
    h1 = h0 - 2
    h2 = h1 - 4
    h3 = h2 - 8
    h4 = h3 - 16
    layer(x_ref, buf_a, h1, 1, k1, b1, 0, False)
    layer(buf_a, buf_b, h2, 2, k2, b2, 1, False)
    layer(buf_b, buf_a, h3, 4, k3, b3, 2, False)
    layer(buf_a, out_ref, h4, 8, kf, bfl, 3, True)


def _kmat(kernel, cin):
    o, c = kernel.shape[:2]
    k = jnp.pad(kernel, ((0, 0), (0, cin - c), (0, 0), (0, 0)))
    return k.transpose(0, 2, 3, 1).reshape(o, 9 * cin)


def run_net(x, lims, layers, out_w, out_ch):
    (k1, b1), (k2, b2), (k3, b3), (kf, bf) = layers
    hid = k1.shape[0]
    h0 = x.shape[0]
    kf_p = jnp.pad(kf, ((0, out_ch - kf.shape[0]), (0, 0), (0, 0), (0, 0)))
    bf_p = jnp.pad(bf, (0, out_ch - bf.shape[0]))
    args = (
        lims, x,
        _kmat(k1, x.shape[1]), b1.reshape(-1, 1),
        _kmat(k2, hid), b2.reshape(-1, 1),
        _kmat(k3, hid), b3.reshape(-1, 1),
        _kmat(kf_p, hid), bf_p.reshape(-1, 1),
    )
    vspec = pl.BlockSpec(memory_space=pltpu.VMEM)
    return pl.pallas_call(
        _net_kernel,
        out_shape=jax.ShapeDtypeStruct((h0 - 30, out_ch, out_w), jnp.bfloat16),
        in_specs=[pl.BlockSpec(memory_space=pltpu.SMEM)] + [vspec] * 9,
        out_specs=vspec,
        scratch_shapes=[
            pltpu.VMEM((h0 - 2, 3 * hid, LANES), jnp.bfloat16),
            pltpu.VMEM((h0 - 6, 3 * hid, LANES), jnp.bfloat16),
        ],
        compiler_params=pltpu.CompilerParams(vmem_limit_bytes=60 * 1024 * 1024),
    )(*args)


def with_halo(cells, width):
    rows = lax.axis_size("row")
    cols = lax.axis_size("col")
    both = ("row", "col")

    def shift(piece, axis, step_r, step_c):
        if axis == "row":
            pairs = [(i, i + step_r) for i in range(rows) if 0 <= i + step_r < rows]
        elif axis == "col":
            pairs = [(j, j + step_c) for j in range(cols) if 0 <= j + step_c < cols]
        else:
            pairs = [
                (i * cols + j, (i + step_r) * cols + j + step_c)
                for i in range(rows)
                for j in range(cols)
                if 0 <= i + step_r < rows and 0 <= j + step_c < cols
            ]
        return lax.ppermute(piece, axis, pairs)

    top = cells[:, :width]
    bottom = cells[:, -width:]
    upper = jnp.concatenate(
        [
            shift(bottom[:, :, -width:], both, 1, 1),
            shift(bottom, "row", 1, 0),
            shift(bottom[:, :, :width], both, 1, -1),
        ],
        axis=2,
    )
    middle = jnp.concatenate(
        [shift(cells[:, :, -width:], "col", 0, 1), cells, shift(cells[:, :, :width], "col", 0, -1)],
        axis=2,
    )
    lower = jnp.concatenate(
        [
            shift(top[:, :, -width:], both, -1, 1),
            shift(top, "row", -1, 0),
            shift(top[:, :, :width], both, -1, -1),
        ],
        axis=2,
    )
    return jnp.concatenate([upper, middle, lower], axis=1)


def body(
    state,
    tile_ids,
    kernel_one,
    bias_one,
    kernel_two,
    bias_two,
    kernel_three,
    bias_three,
    kernel_flux,
    bias_flux,
):
    moments, block_h, block_w = state.shape
    col_count = lax.axis_size("col")
    row_count = lax.axis_size("row")
    my_row = lax.axis_index("row")
    my_col = lax.axis_index("col")
    margin = sum(dilations) + 1
    per_row = block_h // TILE
    per_col = block_w // TILE
    per_block = per_row * per_col
    grid_h = block_h * row_count
    grid_w = block_w * col_count
    layers = (
        (kernel_one, bias_one),
        (kernel_two, bias_two),
        (kernel_three, bias_three),
        (kernel_flux, bias_flux),
    )
    extended = with_halo(state, margin)
    ext_h, ext_w = extended.shape[1:]
    x = jnp.pad(extended.transpose(1, 0, 2), ((0, 0), (0, 16 - moments), (0, LANES - ext_w)))
    lims = []
    offset = margin
    out_h, out_w = ext_h, ext_w
    for spread in dilations:
        offset = offset - spread
        out_h, out_w = out_h - 2 * spread, out_w - 2 * spread
        top = offset - my_row * block_h
        left = offset - my_col * block_w
        lims += [
            jnp.maximum(top, 0),
            jnp.minimum(out_h, grid_h + top),
            jnp.maximum(left, 0),
            jnp.minimum(out_w, grid_w + left),
        ]
    lims = jnp.stack(lims).astype(jnp.int32)
    flux = run_net(x, lims, layers, LANES, 32)[:, : 2 * moments, : block_w + 2].transpose(1, 0, 2)

    every_id = lax.all_gather(tile_ids[0], "row")
    listed = jnp.any(
        every_id[:, :, None] == jnp.arange(col_count * per_block, dtype=jnp.int32)[None, None, :], axis=1
    )
    strip = jnp.array([-1] + [0] * per_row + [1], jnp.int32) + my_row
    tile_row = jnp.array([per_row - 1] + list(range(per_row)) + [0], jnp.int32)
    block = jnp.array([-1] + [0] * per_col + [1], jnp.int32) + my_col
    tile_col = jnp.array([per_col - 1] + list(range(per_col)) + [0], jnp.int32)
    ids = (
        jnp.clip(block, 0, col_count - 1)[None, :] * per_block
        + tile_row[:, None] * per_col
        + tile_col[None, :]
    )
    piece = listed[jnp.clip(strip, 0, row_count - 1)[:, None], ids]
    piece = piece & ((strip >= 0) & (strip < row_count))[:, None] & ((block >= 0) & (block < col_count))[None, :]
    row_sizes = [1] + [TILE] * per_row + [1]
    col_sizes = [1] + [TILE] * per_col + [1]
    cell_mask = jnp.repeat(
        jnp.repeat(piece, jnp.array(row_sizes), axis=0, total_repeat_length=block_h + 2),
        jnp.array(col_sizes),
        axis=1,
        total_repeat_length=block_w + 2,
    )
    rimmed = jnp.where(cell_mask[None], flux, jnp.zeros((), jnp.bfloat16))
    across = rimmed[:moments, 1:-1, :].astype(jnp.float32)
    downward = rimmed[moments:, :, 1:-1].astype(jnp.float32)
    difference = across[:, :, 2:] - across[:, :, :-2] + (downward[:, 2:, :] - downward[:, :-2, :])
    return (-0.5 * difference).astype(jnp.bfloat16)


def solution(mesh):
    return jax.shard_map(
        body,
        mesh=mesh,
        in_specs=(P(None, "row", "col"), P("row", None), P(), P(), P(), P(), P(), P(), P(), P()),
        out_specs=P(None, "row", "col"),
        check_vma=False,
    )
```

```python
import jax
import jax.numpy as jnp
from jax import lax
from jax.experimental import pallas as pl
from jax.experimental.pallas import tpu as pltpu
from jax.sharding import PartitionSpec as P

TILE = 64


dilations = (1, 2, 4, 8)
LANES = 384


def _net_kernel(lim_ref, x_ref, k1, b1, k2, b2, k3, b3, kf, bfl, out_ref, buf_a, buf_b):
    lanes = lax.broadcasted_iota(jnp.int32, (1, LANES), 1)

    def layer(src, dst, n_rows, spread, kmat, bias, index, last):
        kv = kmat[...]
        bv = bias[...]
        if not last:
            after = dilations[index + 1]
            row_lo = lim_ref[4 * index]
            row_hi = lim_ref[4 * index + 1]
            col_ok = (lanes >= lim_ref[4 * index + 2]) & (lanes < lim_ref[4 * index + 3])

        def row(y, carry):
            pieces = []
            for a in range(3):
                line = src[y + spread * a]
                if index == 0:
                    for e in range(3):
                        pieces.append(line if e == 0 else pltpu.roll(line, LANES - spread * e, 1))
                else:
                    pieces.append(line)
            col = jnp.concatenate(pieces, axis=0)
            acc = jnp.dot(kv, col, preferred_element_type=jnp.float32) + bv
            if last:
                dst[y] = acc[:, : dst.shape[2]].astype(dst.dtype)
            else:
                half = 0.5 * acc
                act = half + half * jnp.tanh(half)
                keep = col_ok & (y >= row_lo) & (y < row_hi)
                kept = jnp.where(keep, act, 0.0).astype(dst.dtype)
                dst[y] = jnp.concatenate(
                    [kept] + [pltpu.roll(kept, LANES - after * e, 1) for e in (1, 2)], axis=0
                )
            return carry

        lax.fori_loop(0, n_rows, row, 0, unroll=2)

    h0 = x_ref.shape[0]
    h1 = h0 - 2
    h2 = h1 - 4
    h3 = h2 - 8
    h4 = h3 - 16
    layer(x_ref, buf_a, h1, 1, k1, b1, 0, False)
    layer(buf_a, buf_b, h2, 2, k2, b2, 1, False)
    layer(buf_b, buf_a, h3, 4, k3, b3, 2, False)
    layer(buf_a, out_ref, h4, 8, kf, bfl, 3, True)


def _kmat(kernel, cin):
    o, c = kernel.shape[:2]
    k = jnp.pad(kernel, ((0, 0), (0, cin - c), (0, 0), (0, 0)))
    return k.transpose(0, 2, 3, 1).reshape(o, 9 * cin)


def run_net(x, lims, layers, out_w, out_ch):
    (k1, b1), (k2, b2), (k3, b3), (kf, bf) = layers
    hid = k1.shape[0]
    h0 = x.shape[0]
    kf_p = jnp.pad(kf, ((0, out_ch - kf.shape[0]), (0, 0), (0, 0), (0, 0)))
    bf_p = jnp.pad(bf, (0, out_ch - bf.shape[0]))
    args = (
        lims, x,
        _kmat(k1, x.shape[1]), b1.reshape(-1, 1),
        _kmat(k2, hid), b2.reshape(-1, 1),
        _kmat(k3, hid), b3.reshape(-1, 1),
        _kmat(kf_p, hid), bf_p.reshape(-1, 1),
    )
    vspec = pl.BlockSpec(memory_space=pltpu.VMEM)
    return pl.pallas_call(
        _net_kernel,
        out_shape=jax.ShapeDtypeStruct((h0 - 30, out_ch, out_w), jnp.bfloat16),
        in_specs=[pl.BlockSpec(memory_space=pltpu.SMEM)] + [vspec] * 9,
        out_specs=vspec,
        scratch_shapes=[
            pltpu.VMEM((h0 - 2, 3 * hid, LANES), jnp.bfloat16),
            pltpu.VMEM((h0 - 6, 3 * hid, LANES), jnp.bfloat16),
        ],
        compiler_params=pltpu.CompilerParams(vmem_limit_bytes=60 * 1024 * 1024),
    )(*args)


def with_halo(cells, width):
    rows = lax.axis_size("row")
    cols = lax.axis_size("col")
    both = ("row", "col")

    def shift(piece, axis, step_r, step_c):
        if axis == "row":
            pairs = [(i, i + step_r) for i in range(rows) if 0 <= i + step_r < rows]
        elif axis == "col":
            pairs = [(j, j + step_c) for j in range(cols) if 0 <= j + step_c < cols]
        else:
            pairs = [
                (i * cols + j, (i + step_r) * cols + j + step_c)
                for i in range(rows)
                for j in range(cols)
                if 0 <= i + step_r < rows and 0 <= j + step_c < cols
            ]
        return lax.ppermute(piece, axis, pairs)

    top = cells[:, :width]
    bottom = cells[:, -width:]
    upper = jnp.concatenate(
        [
            shift(bottom[:, :, -width:], both, 1, 1),
            shift(bottom, "row", 1, 0),
            shift(bottom[:, :, :width], both, 1, -1),
        ],
        axis=2,
    )
    middle = jnp.concatenate(
        [shift(cells[:, :, -width:], "col", 0, 1), cells, shift(cells[:, :, :width], "col", 0, -1)],
        axis=2,
    )
    lower = jnp.concatenate(
        [
            shift(top[:, :, -width:], both, -1, 1),
            shift(top, "row", -1, 0),
            shift(top[:, :, :width], both, -1, -1),
        ],
        axis=2,
    )
    return jnp.concatenate([upper, middle, lower], axis=1)


def body(
    state,
    tile_ids,
    kernel_one,
    bias_one,
    kernel_two,
    bias_two,
    kernel_three,
    bias_three,
    kernel_flux,
    bias_flux,
):
    moments, block_h, block_w = state.shape
    col_count = lax.axis_size("col")
    row_count = lax.axis_size("row")
    my_row = lax.axis_index("row")
    my_col = lax.axis_index("col")
    margin = sum(dilations) + 1
    per_row = block_h // TILE
    per_col = block_w // TILE
    per_block = per_row * per_col
    grid_h = block_h * row_count
    grid_w = block_w * col_count
    layers = (
        (kernel_one, bias_one),
        (kernel_two, bias_two),
        (kernel_three, bias_three),
        (kernel_flux, bias_flux),
    )
    extended = with_halo(state, margin)
    ext_h, ext_w = extended.shape[1:]
    x = jnp.pad(extended.transpose(1, 0, 2), ((0, 0), (0, 16 - moments), (0, LANES - ext_w)))
    lims = []
    offset = margin
    out_h, out_w = ext_h, ext_w
    for spread in dilations:
        offset = offset - spread
        out_h, out_w = out_h - 2 * spread, out_w - 2 * spread
        top = offset - my_row * block_h
        left = offset - my_col * block_w
        lims += [
            jnp.maximum(top, 0),
            jnp.minimum(out_h, grid_h + top),
            jnp.maximum(left, 0),
            jnp.minimum(out_w, grid_w + left),
        ]
    lims = jnp.stack(lims).astype(jnp.int32)
    flux = run_net(x, lims, layers, LANES, 32)[:, : 2 * moments, : block_w + 2].transpose(1, 0, 2)

    near_ids = jnp.concatenate(
        [
            lax.ppermute(tile_ids, "row", [(i, i + 1) for i in range(row_count - 1)]),
            tile_ids,
            lax.ppermute(tile_ids, "row", [(i + 1, i) for i in range(row_count - 1)]),
        ],
        axis=0,
    )
    listed = jnp.any(
        near_ids[:, :, None] == jnp.arange(col_count * per_block, dtype=jnp.int32)[None, None, :], axis=1
    )
    strip = jnp.array([-1] + [0] * per_row + [1], jnp.int32)
    tile_row = jnp.array([per_row - 1] + list(range(per_row)) + [0], jnp.int32)
    block = jnp.array([-1] + [0] * per_col + [1], jnp.int32) + my_col
    tile_col = jnp.array([per_col - 1] + list(range(per_col)) + [0], jnp.int32)
    ids = (
        jnp.clip(block, 0, col_count - 1)[None, :] * per_block
        + tile_row[:, None] * per_col
        + tile_col[None, :]
    )
    piece = listed[(strip + 1)[:, None], ids]
    strip = strip + my_row
    piece = piece & ((strip >= 0) & (strip < row_count))[:, None] & ((block >= 0) & (block < col_count))[None, :]
    row_sizes = [1] + [TILE] * per_row + [1]
    col_sizes = [1] + [TILE] * per_col + [1]
    cell_mask = jnp.repeat(
        jnp.repeat(piece, jnp.array(row_sizes), axis=0, total_repeat_length=block_h + 2),
        jnp.array(col_sizes),
        axis=1,
        total_repeat_length=block_w + 2,
    )
    rimmed = jnp.where(cell_mask[None], flux, jnp.zeros((), jnp.bfloat16))
    across = rimmed[:moments, 1:-1, :].astype(jnp.float32)
    downward = rimmed[moments:, :, 1:-1].astype(jnp.float32)
    difference = across[:, :, 2:] - across[:, :, :-2] + (downward[:, 2:, :] - downward[:, :-2, :])
    return (-0.5 * difference).astype(jnp.bfloat16)


def solution(mesh):
    return jax.shard_map(
        body,
        mesh=mesh,
        in_specs=(P(None, "row", "col"), P("row", None), P(), P(), P(), P(), P(), P(), P(), P()),
        out_specs=P(None, "row", "col"),
        check_vma=False,
    )
```

```python
import jax
import jax.numpy as jnp
from jax import lax
from jax.experimental import pallas as pl
from jax.experimental.pallas import tpu as pltpu
from jax.sharding import PartitionSpec as P

TILE = 64


dilations = (1, 2, 4, 8)
LANES = 384


def _net_kernel(lim_ref, x_ref, k1, b1, k2, b2, k3, b3, kf, bfl, out_ref, buf_a, buf_b):
    lanes = lax.broadcasted_iota(jnp.int32, (1, LANES), 1)

    def layer(src, dst, n_rows, spread, kmat, bias, index, last):
        kv = kmat[...]
        bv = bias[...]
        if not last:
            after = dilations[index + 1]
            row_lo = lim_ref[4 * index]
            row_hi = lim_ref[4 * index + 1]
            col_ok = (lanes >= lim_ref[4 * index + 2]) & (lanes < lim_ref[4 * index + 3])

        def row(y, carry):
            pieces = []
            for a in range(3):
                line = src[y + spread * a]
                if index == 0:
                    for e in range(3):
                        pieces.append(line if e == 0 else pltpu.roll(line, LANES - spread * e, 1))
                else:
                    pieces.append(line)
            col = jnp.concatenate(pieces, axis=0)
            acc = jnp.dot(kv, col, preferred_element_type=jnp.float32) + bv
            if last:
                dst[y] = acc[:, : dst.shape[2]].astype(dst.dtype)
            else:
                half = 0.5 * acc
                act = half + half * jnp.tanh(half)
                keep = col_ok & (y >= row_lo) & (y < row_hi)
                kept = jnp.where(keep, act, 0.0).astype(dst.dtype)
                dst[y] = jnp.concatenate(
                    [kept] + [pltpu.roll(kept, LANES - after * e, 1) for e in (1, 2)], axis=0
                )
            return carry

        lax.fori_loop(0, n_rows, row, 0, unroll=2)

    h0 = x_ref.shape[0]
    h1 = h0 - 2
    h2 = h1 - 4
    h3 = h2 - 8
    h4 = h3 - 16
    layer(x_ref, buf_a, h1, 1, k1, b1, 0, False)
    layer(buf_a, buf_b, h2, 2, k2, b2, 1, False)
    layer(buf_b, buf_a, h3, 4, k3, b3, 2, False)
    layer(buf_a, out_ref, h4, 8, kf, bfl, 3, True)


def _kmat(kernel, cin):
    o, c = kernel.shape[:2]
    k = jnp.pad(kernel, ((0, 0), (0, cin - c), (0, 0), (0, 0)))
    return k.transpose(0, 2, 3, 1).reshape(o, 9 * cin)


def run_net(x, lims, layers, out_w, out_ch):
    (k1, b1), (k2, b2), (k3, b3), (kf, bf) = layers
    hid = k1.shape[0]
    h0 = x.shape[0]
    kf_p = jnp.pad(kf, ((0, out_ch - kf.shape[0]), (0, 0), (0, 0), (0, 0)))
    bf_p = jnp.pad(bf, (0, out_ch - bf.shape[0]))
    args = (
        lims, x,
        _kmat(k1, x.shape[1]), b1.reshape(-1, 1),
        _kmat(k2, hid), b2.reshape(-1, 1),
        _kmat(k3, hid), b3.reshape(-1, 1),
        _kmat(kf_p, hid), bf_p.reshape(-1, 1),
    )
    vspec = pl.BlockSpec(memory_space=pltpu.VMEM)
    return pl.pallas_call(
        _net_kernel,
        out_shape=jax.ShapeDtypeStruct((h0 - 30, out_ch, out_w), jnp.bfloat16),
        in_specs=[pl.BlockSpec(memory_space=pltpu.SMEM)] + [vspec] * 9,
        out_specs=vspec,
        scratch_shapes=[
            pltpu.VMEM((h0 - 2, 3 * hid, LANES), jnp.bfloat16),
            pltpu.VMEM((h0 - 6, 3 * hid, LANES), jnp.bfloat16),
        ],
        compiler_params=pltpu.CompilerParams(vmem_limit_bytes=60 * 1024 * 1024),
    )(*args)


def with_halo(cells, sides, width):
    for axis, dim in sides:
        count = lax.axis_size(axis)
        ends = count - 1
        head = lax.slice_in_dim(cells, 0, width, axis=dim)
        tail = lax.slice_in_dim(cells, cells.shape[dim] - width, cells.shape[dim], axis=dim)
        cells = jnp.concatenate(
            [
                lax.ppermute(tail, axis, [(i, (i + 1) % count) for i in range(ends)]),
                cells,
                lax.ppermute(head, axis, [((i + 1) % count, i) for i in range(ends)]),
            ],
            axis=dim,
        )
    return cells


def body(
    state,
    tile_ids,
    kernel_one,
    bias_one,
    kernel_two,
    bias_two,
    kernel_three,
    bias_three,
    kernel_flux,
    bias_flux,
):
    moments, block_h, block_w = state.shape
    col_count = lax.axis_size("col")
    row_count = lax.axis_size("row")
    my_row = lax.axis_index("row")
    my_col = lax.axis_index("col")
    margin = sum(dilations) + 1
    per_row = block_h // TILE
    per_col = block_w // TILE
    per_block = per_row * per_col
    grid_h = block_h * row_count
    grid_w = block_w * col_count
    layers = (
        (kernel_one, bias_one),
        (kernel_two, bias_two),
        (kernel_three, bias_three),
        (kernel_flux, bias_flux),
    )
    extended = with_halo(state, (("row", 1), ("col", 2)), margin)
    ext_h, ext_w = extended.shape[1:]
    x = jnp.pad(extended.transpose(1, 0, 2), ((0, 0), (0, 16 - moments), (0, LANES - ext_w)))
    lims = []
    offset = margin
    out_h, out_w = ext_h, ext_w
    for spread in dilations:
        offset = offset - spread
        out_h, out_w = out_h - 2 * spread, out_w - 2 * spread
        top = offset - my_row * block_h
        left = offset - my_col * block_w
        lims += [
            jnp.maximum(top, 0),
            jnp.minimum(out_h, grid_h + top),
            jnp.maximum(left, 0),
            jnp.minimum(out_w, grid_w + left),
        ]
    lims = jnp.stack(lims).astype(jnp.int32)
    flux = run_net(x, lims, layers, LANES, 32)[:, : 2 * moments, : block_w + 2].transpose(1, 0, 2)

    near_ids = jnp.concatenate(
        [
            lax.ppermute(tile_ids, "row", [(i, i + 1) for i in range(row_count - 1)]),
            tile_ids,
            lax.ppermute(tile_ids, "row", [(i + 1, i) for i in range(row_count - 1)]),
        ],
        axis=0,
    )
    listed = jnp.any(
        near_ids[:, :, None] == jnp.arange(col_count * per_block, dtype=jnp.int32)[None, None, :], axis=1
    )
    strip = jnp.array([-1] + [0] * per_row + [1], jnp.int32)
    tile_row = jnp.array([per_row - 1] + list(range(per_row)) + [0], jnp.int32)
    block = jnp.array([-1] + [0] * per_col + [1], jnp.int32) + my_col
    tile_col = jnp.array([per_col - 1] + list(range(per_col)) + [0], jnp.int32)
    ids = (
        jnp.clip(block, 0, col_count - 1)[None, :] * per_block
        + tile_row[:, None] * per_col
        + tile_col[None, :]
    )
    piece = listed[(strip + 1)[:, None], ids]
    strip = strip + my_row
    piece = piece & ((strip >= 0) & (strip < row_count))[:, None] & ((block >= 0) & (block < col_count))[None, :]
    row_sizes = [1] + [TILE] * per_row + [1]
    col_sizes = [1] + [TILE] * per_col + [1]
    cell_mask = jnp.repeat(
        jnp.repeat(piece, jnp.array(row_sizes), axis=0, total_repeat_length=block_h + 2),
        jnp.array(col_sizes),
        axis=1,
        total_repeat_length=block_w + 2,
    )
    rimmed = jnp.where(cell_mask[None], flux, jnp.zeros((), jnp.bfloat16))
    across = rimmed[:moments, 1:-1, :].astype(jnp.float32)
    downward = rimmed[moments:, :, 1:-1].astype(jnp.float32)
    difference = across[:, :, 2:] - across[:, :, :-2] + (downward[:, 2:, :] - downward[:, :-2, :])
    return (-0.5 * difference).astype(jnp.bfloat16)


def solution(mesh):
    return jax.shard_map(
        body,
        mesh=mesh,
        in_specs=(P(None, "row", "col"), P("row", None), P(), P(), P(), P(), P(), P(), P(), P()),
        out_specs=P(None, "row", "col"),
        check_vma=False,
    )
```

```python
import jax
import jax.numpy as jnp
from jax import lax
from jax.experimental import pallas as pl
from jax.experimental.pallas import tpu as pltpu
from jax.sharding import PartitionSpec as P

TILE = 64


dilations = (1, 2, 4, 8)
LANES = 384


def _net_kernel(lim_ref, x_ref, k1, b1, k2, b2, k3, b3, kf, bfl, out_ref, buf_a, buf_b):
    lanes = lax.broadcasted_iota(jnp.int32, (1, LANES), 1)

    def layer(src, dst, n_rows, spread, kmat, bias, index, last):
        kv = kmat[...]
        bv = bias[...]
        if not last:
            after = dilations[index + 1]
            row_lo = lim_ref[4 * index]
            row_hi = lim_ref[4 * index + 1]
            col_ok = (lanes >= lim_ref[4 * index + 2]) & (lanes < lim_ref[4 * index + 3])

        def row(y, carry):
            pieces = []
            for a in range(3):
                line = src[y + spread * a]
                if index == 0:
                    for e in range(3):
                        pieces.append(line if e == 0 else pltpu.roll(line, LANES - spread * e, 1))
                else:
                    pieces.append(line)
            col = jnp.concatenate(pieces, axis=0)
            acc = jnp.dot(kv, col, preferred_element_type=jnp.float32) + bv
            if last:
                dst[y] = acc[:, : dst.shape[2]].astype(dst.dtype)
            else:
                half = 0.5 * acc
                act = half + half * jnp.tanh(half)
                keep = col_ok & (y >= row_lo) & (y < row_hi)
                kept = jnp.where(keep, act, 0.0).astype(dst.dtype)
                dst[y] = jnp.concatenate(
                    [kept] + [pltpu.roll(kept, LANES - after * e, 1) for e in (1, 2)], axis=0
                )
            return carry

        lax.fori_loop(0, n_rows, row, 0, unroll=8)

    h0 = x_ref.shape[0]
    h1 = h0 - 2
    h2 = h1 - 4
    h3 = h2 - 8
    h4 = h3 - 16
    layer(x_ref, buf_a, h1, 1, k1, b1, 0, False)
    layer(buf_a, buf_b, h2, 2, k2, b2, 1, False)
    layer(buf_b, buf_a, h3, 4, k3, b3, 2, False)
    layer(buf_a, out_ref, h4, 8, kf, bfl, 3, True)


def _kmat(kernel, cin):
    o, c = kernel.shape[:2]
    k = jnp.pad(kernel, ((0, 0), (0, cin - c), (0, 0), (0, 0)))
    return k.transpose(0, 2, 3, 1).reshape(o, 9 * cin)


def run_net(x, lims, layers, out_w, out_ch):
    (k1, b1), (k2, b2), (k3, b3), (kf, bf) = layers
    hid = k1.shape[0]
    h0 = x.shape[0]
    kf_p = jnp.pad(kf, ((0, out_ch - kf.shape[0]), (0, 0), (0, 0), (0, 0)))
    bf_p = jnp.pad(bf, (0, out_ch - bf.shape[0]))
    args = (
        lims, x,
        _kmat(k1, x.shape[1]), b1.reshape(-1, 1),
        _kmat(k2, hid), b2.reshape(-1, 1),
        _kmat(k3, hid), b3.reshape(-1, 1),
        _kmat(kf_p, hid), bf_p.reshape(-1, 1),
    )
    vspec = pl.BlockSpec(memory_space=pltpu.VMEM)
    return pl.pallas_call(
        _net_kernel,
        out_shape=jax.ShapeDtypeStruct((h0 - 30, out_ch, out_w), jnp.bfloat16),
        in_specs=[pl.BlockSpec(memory_space=pltpu.SMEM)] + [vspec] * 9,
        out_specs=vspec,
        scratch_shapes=[
            pltpu.VMEM((h0 - 2, 3 * hid, LANES), jnp.bfloat16),
            pltpu.VMEM((h0 - 6, 3 * hid, LANES), jnp.bfloat16),
        ],
        compiler_params=pltpu.CompilerParams(vmem_limit_bytes=60 * 1024 * 1024),
    )(*args)


def with_halo(cells, sides, width):
    for axis, dim in sides:
        count = lax.axis_size(axis)
        ends = count - 1
        head = lax.slice_in_dim(cells, 0, width, axis=dim)
        tail = lax.slice_in_dim(cells, cells.shape[dim] - width, cells.shape[dim], axis=dim)
        cells = jnp.concatenate(
            [
                lax.ppermute(tail, axis, [(i, (i + 1) % count) for i in range(ends)]),
                cells,
                lax.ppermute(head, axis, [((i + 1) % count, i) for i in range(ends)]),
            ],
            axis=dim,
        )
    return cells


def body(
    state,
    tile_ids,
    kernel_one,
    bias_one,
    kernel_two,
    bias_two,
    kernel_three,
    bias_three,
    kernel_flux,
    bias_flux,
):
    moments, block_h, block_w = state.shape
    col_count = lax.axis_size("col")
    row_count = lax.axis_size("row")
    my_row = lax.axis_index("row")
    my_col = lax.axis_index("col")
    margin = sum(dilations) + 1
    per_row = block_h // TILE
    per_col = block_w // TILE
    per_block = per_row * per_col
    grid_h = block_h * row_count
    grid_w = block_w * col_count
    layers = (
        (kernel_one, bias_one),
        (kernel_two, bias_two),
        (kernel_three, bias_three),
        (kernel_flux, bias_flux),
    )
    extended = with_halo(state, (("row", 1), ("col", 2)), margin)
    ext_h, ext_w = extended.shape[1:]
    x = jnp.pad(extended.transpose(1, 0, 2), ((0, 0), (0, 16 - moments), (0, LANES - ext_w)))
    lims = []
    offset = margin
    out_h, out_w = ext_h, ext_w
    for spread in dilations:
        offset = offset - spread
        out_h, out_w = out_h - 2 * spread, out_w - 2 * spread
        top = offset - my_row * block_h
        left = offset - my_col * block_w
        lims += [
            jnp.maximum(top, 0),
            jnp.minimum(out_h, grid_h + top),
            jnp.maximum(left, 0),
            jnp.minimum(out_w, grid_w + left),
        ]
    lims = jnp.stack(lims).astype(jnp.int32)

    x, late_ids = lax.optimization_barrier((x, tile_ids))
    near_ids = jnp.concatenate(
        [
            lax.ppermute(late_ids, "row", [(i, i + 1) for i in range(row_count - 1)]),
            tile_ids,
            lax.ppermute(late_ids, "row", [(i + 1, i) for i in range(row_count - 1)]),
        ],
        axis=0,
    )
    flux = run_net(x, lims, layers, LANES, 32)[:, : 2 * moments, : block_w + 2].transpose(1, 0, 2)
    listed = jnp.any(
        near_ids[:, :, None] == jnp.arange(col_count * per_block, dtype=jnp.int32)[None, None, :], axis=1
    )
    strip = jnp.array([-1] + [0] * per_row + [1], jnp.int32)
    tile_row = jnp.array([per_row - 1] + list(range(per_row)) + [0], jnp.int32)
    block = jnp.array([-1] + [0] * per_col + [1], jnp.int32) + my_col
    tile_col = jnp.array([per_col - 1] + list(range(per_col)) + [0], jnp.int32)
    ids = (
        jnp.clip(block, 0, col_count - 1)[None, :] * per_block
        + tile_row[:, None] * per_col
        + tile_col[None, :]
    )
    piece = listed[(strip + 1)[:, None], ids]
    strip = strip + my_row
    piece = piece & ((strip >= 0) & (strip < row_count))[:, None] & ((block >= 0) & (block < col_count))[None, :]
    row_sizes = [1] + [TILE] * per_row + [1]
    col_sizes = [1] + [TILE] * per_col + [1]
    cell_mask = jnp.repeat(
        jnp.repeat(piece, jnp.array(row_sizes), axis=0, total_repeat_length=block_h + 2),
        jnp.array(col_sizes),
        axis=1,
        total_repeat_length=block_w + 2,
    )
    rimmed = jnp.where(cell_mask[None], flux, jnp.zeros((), jnp.bfloat16))
    across = rimmed[:moments, 1:-1, :].astype(jnp.float32)
    downward = rimmed[moments:, :, 1:-1].astype(jnp.float32)
    difference = across[:, :, 2:] - across[:, :, :-2] + (downward[:, 2:, :] - downward[:, :-2, :])
    return (-0.5 * difference).astype(jnp.bfloat16)


def solution(mesh):
    return jax.shard_map(
        body,
        mesh=mesh,
        in_specs=(P(None, "row", "col"), P("row", None), P(), P(), P(), P(), P(), P(), P(), P()),
        out_specs=P(None, "row", "col"),
        check_vma=False,
    )
```

```python
import jax
import jax.numpy as jnp
from jax import lax
from jax.experimental import pallas as pl
from jax.experimental.pallas import tpu as pltpu
from jax.sharding import PartitionSpec as P

TILE = 64


dilations = (1, 2, 4, 8)
LANES = 384


def _net_kernel(lim_ref, x_ref, k1, b1, k2, b2, k3, b3, kf, bfl, out_ref, buf_a, buf_b):
    lanes = lax.broadcasted_iota(jnp.int32, (1, LANES), 1)

    def layer(src, dst, n_rows, spread, kmat, bias, index, last):
        kv = kmat[...]
        bv = bias[...]
        if not last:
            after = dilations[index + 1]
            row_lo = lim_ref[4 * index]
            row_hi = lim_ref[4 * index + 1]
            col_ok = (lanes >= lim_ref[4 * index + 2]) & (lanes < lim_ref[4 * index + 3])

        def row(y, carry):
            pieces = []
            for a in range(3):
                line = src[y + spread * a]
                if index == 0:
                    for e in range(3):
                        pieces.append(line if e == 0 else pltpu.roll(line, LANES - spread * e, 1))
                else:
                    pieces.append(line)
            col = jnp.concatenate(pieces, axis=0)
            acc = jnp.dot(kv, col, preferred_element_type=jnp.float32) + bv
            if last:
                dst[y] = acc[:, : dst.shape[2]].astype(dst.dtype)
            else:
                half = 0.5 * acc
                act = half + half * jnp.tanh(half)
                keep = col_ok & (y >= row_lo) & (y < row_hi)
                kept = jnp.where(keep, act, 0.0).astype(dst.dtype)
                dst[y] = jnp.concatenate(
                    [kept] + [pltpu.roll(kept, LANES - after * e, 1) for e in (1, 2)], axis=0
                )
            return carry

        lax.fori_loop(0, n_rows, row, 0, unroll=8)

    h0 = x_ref.shape[0]
    h1 = h0 - 2
    h2 = h1 - 4
    h3 = h2 - 8
    h4 = h3 - 16
    layer(x_ref, buf_a, h1, 1, k1, b1, 0, False)
    layer(buf_a, buf_b, h2, 2, k2, b2, 1, False)
    layer(buf_b, buf_a, h3, 4, k3, b3, 2, False)
    layer(buf_a, out_ref, h4, 8, kf, bfl, 3, True)


def _kmat(kernel, cin):
    o, c = kernel.shape[:2]
    k = jnp.pad(kernel, ((0, 0), (0, cin - c), (0, 0), (0, 0)))
    return k.transpose(0, 2, 3, 1).reshape(o, 9 * cin)


def run_net(x, lims, layers, out_w, out_ch):
    (k1, b1), (k2, b2), (k3, b3), (kf, bf) = layers
    hid = k1.shape[0]
    h0 = x.shape[0]
    kf_p = jnp.pad(kf, ((0, out_ch - kf.shape[0]), (0, 0), (0, 0), (0, 0)))
    bf_p = jnp.pad(bf, (0, out_ch - bf.shape[0]))
    args = (
        lims, x,
        _kmat(k1, x.shape[1]), b1.reshape(-1, 1),
        _kmat(k2, hid), b2.reshape(-1, 1),
        _kmat(k3, hid), b3.reshape(-1, 1),
        _kmat(kf_p, hid), bf_p.reshape(-1, 1),
    )
    vspec = pl.BlockSpec(memory_space=pltpu.VMEM)
    return pl.pallas_call(
        _net_kernel,
        out_shape=jax.ShapeDtypeStruct((h0 - 30, out_ch, out_w), jnp.bfloat16),
        in_specs=[pl.BlockSpec(memory_space=pltpu.SMEM)] + [vspec] * 9,
        out_specs=vspec,
        scratch_shapes=[
            pltpu.VMEM((h0 - 2, 3 * hid, LANES), jnp.bfloat16),
            pltpu.VMEM((h0 - 6, 3 * hid, LANES), jnp.bfloat16),
        ],
        compiler_params=pltpu.CompilerParams(vmem_limit_bytes=60 * 1024 * 1024),
    )(*args)


def with_halo(cells, sides, width):
    for axis, dim in sides:
        count = lax.axis_size(axis)
        ends = count - 1
        head = lax.slice_in_dim(cells, 0, width, axis=dim)
        tail = lax.slice_in_dim(cells, cells.shape[dim] - width, cells.shape[dim], axis=dim)
        cells = jnp.concatenate(
            [
                lax.ppermute(tail, axis, [(i, (i + 1) % count) for i in range(ends)]),
                cells,
                lax.ppermute(head, axis, [((i + 1) % count, i) for i in range(ends)]),
            ],
            axis=dim,
        )
    return cells


def body(
    state,
    tile_ids,
    kernel_one,
    bias_one,
    kernel_two,
    bias_two,
    kernel_three,
    bias_three,
    kernel_flux,
    bias_flux,
):
    moments, block_h, block_w = state.shape
    col_count = lax.axis_size("col")
    row_count = lax.axis_size("row")
    my_row = lax.axis_index("row")
    my_col = lax.axis_index("col")
    margin = sum(dilations) + 1
    per_row = block_h // TILE
    per_col = block_w // TILE
    per_block = per_row * per_col
    grid_h = block_h * row_count
    grid_w = block_w * col_count
    layers = (
        (kernel_one, bias_one),
        (kernel_two, bias_two),
        (kernel_three, bias_three),
        (kernel_flux, bias_flux),
    )
    listed = tile_ids[0]
    mine = (listed // per_block) == my_col
    local_ids = listed % per_block
    chosen = jnp.any(
        mine[None, :] & (local_ids[None, :] == jnp.arange(per_block, dtype=jnp.int32)[:, None]), axis=1
    )
    own_mask = jnp.broadcast_to(
        chosen.reshape(per_row, 1, per_col, 1), (per_row, TILE, per_col, TILE)
    ).reshape(1, block_h, block_w)
    marked = jnp.concatenate([state, own_mask.astype(state.dtype)], axis=0)
    extended = with_halo(marked, (("row", 1), ("col", 2)), margin)
    ext_h, ext_w = extended.shape[1:]
    x = jnp.pad(extended.transpose(1, 0, 2), ((0, 0), (0, 15 - moments), (0, LANES - ext_w)))
    lims = []
    offset = margin
    out_h, out_w = ext_h, ext_w
    for spread in dilations:
        offset = offset - spread
        out_h, out_w = out_h - 2 * spread, out_w - 2 * spread
        top = offset - my_row * block_h
        left = offset - my_col * block_w
        lims += [
            jnp.maximum(top, 0),
            jnp.minimum(out_h, grid_h + top),
            jnp.maximum(left, 0),
            jnp.minimum(out_w, grid_w + left),
        ]
    lims = jnp.stack(lims).astype(jnp.int32)

    flux = run_net(x, lims, layers, LANES, 32)[:, : 2 * moments, : block_w + 2].transpose(1, 0, 2)
    cell_mask = extended[moments, margin - 1 : margin + block_h + 1, margin - 1 : margin + block_w + 1] > 0
    rimmed = jnp.where(cell_mask[None], flux, jnp.zeros((), jnp.bfloat16))
    across = rimmed[:moments, 1:-1, :].astype(jnp.float32)
    downward = rimmed[moments:, :, 1:-1].astype(jnp.float32)
    difference = across[:, :, 2:] - across[:, :, :-2] + (downward[:, 2:, :] - downward[:, :-2, :])
    return (-0.5 * difference).astype(jnp.bfloat16)


def solution(mesh):
    return jax.shard_map(
        body,
        mesh=mesh,
        in_specs=(P(None, "row", "col"), P("row", None), P(), P(), P(), P(), P(), P(), P(), P()),
        out_specs=P(None, "row", "col"),
        check_vma=False,
    )
```

```python
import jax
import jax.numpy as jnp
from jax import lax
from jax.experimental import pallas as pl
from jax.experimental.pallas import tpu as pltpu
from jax.sharding import PartitionSpec as P

TILE = 64


dilations = (1, 2, 4, 8)
LANES = 384


def _net_kernel(lim_ref, x_ref, k1, b1, k2, b2, k3, b3, kf, bfl, out_ref, buf_a, buf_b):
    lanes = lax.broadcasted_iota(jnp.int32, (1, LANES), 1)

    def layer(src, dst, n_rows, spread, kmat, bias, index, last):
        kv = kmat[...]
        bv = bias[...]
        if not last:
            after = dilations[index + 1]
            row_lo = lim_ref[4 * index]
            row_hi = lim_ref[4 * index + 1]
            col_ok = (lanes >= lim_ref[4 * index + 2]) & (lanes < lim_ref[4 * index + 3])

        def row(y, carry):
            pieces = []
            for a in range(3):
                line = src[y + spread * a]
                if index == 0:
                    for e in range(3):
                        pieces.append(line if e == 0 else pltpu.roll(line, LANES - spread * e, 1))
                else:
                    pieces.append(line)
            col = jnp.concatenate(pieces, axis=0)
            acc = jnp.dot(kv, col, preferred_element_type=jnp.float32) + bv
            if last:
                dst[y] = acc[:, : dst.shape[2]].astype(dst.dtype)
            else:
                half = 0.5 * acc
                act = half + half * jnp.tanh(half)
                keep = col_ok & (y >= row_lo) & (y < row_hi)
                kept = jnp.where(keep, act, 0.0).astype(dst.dtype)
                dst[y] = jnp.concatenate(
                    [kept] + [pltpu.roll(kept, LANES - after * e, 1) for e in (1, 2)], axis=0
                )
            return carry

        lax.fori_loop(0, n_rows, row, 0, unroll=8)

    h0 = x_ref.shape[0]
    h1 = h0 - 2
    h2 = h1 - 4
    h3 = h2 - 8
    h4 = h3 - 16
    layer(x_ref, buf_a, h1, 1, k1, b1, 0, False)
    layer(buf_a, buf_b, h2, 2, k2, b2, 1, False)
    layer(buf_b, buf_a, h3, 4, k3, b3, 2, False)
    layer(buf_a, out_ref, h4, 8, kf, bfl, 3, True)


def _kmat(kernel, cin):
    o, c = kernel.shape[:2]
    k = jnp.pad(kernel, ((0, 0), (0, cin - c), (0, 0), (0, 0)))
    return k.transpose(0, 2, 3, 1).reshape(o, 9 * cin)


def run_net(x, lims, layers, out_w, out_ch):
    (k1, b1), (k2, b2), (k3, b3), (kf, bf) = layers
    hid = k1.shape[0]
    h0 = x.shape[0]
    kf_p = jnp.pad(kf, ((0, out_ch - kf.shape[0]), (0, 0), (0, 0), (0, 0)))
    bf_p = jnp.pad(bf, (0, out_ch - bf.shape[0]))
    args = (
        lims, x,
        _kmat(k1, x.shape[1]), b1.reshape(-1, 1),
        _kmat(k2, hid), b2.reshape(-1, 1),
        _kmat(k3, hid), b3.reshape(-1, 1),
        _kmat(kf_p, hid), bf_p.reshape(-1, 1),
    )
    vspec = pl.BlockSpec(memory_space=pltpu.VMEM)
    return pl.pallas_call(
        _net_kernel,
        out_shape=jax.ShapeDtypeStruct((h0 - 30, out_ch, out_w), jnp.bfloat16),
        in_specs=[pl.BlockSpec(memory_space=pltpu.SMEM)] + [vspec] * 9,
        out_specs=vspec,
        scratch_shapes=[
            pltpu.VMEM((h0 - 2, 3 * hid, LANES), jnp.bfloat16),
            pltpu.VMEM((h0 - 6, 3 * hid, LANES), jnp.bfloat16),
        ],
        compiler_params=pltpu.CompilerParams(vmem_limit_bytes=60 * 1024 * 1024),
    )(*args)


def with_halo(cells, sides, width):
    for axis, dim in sides:
        count = lax.axis_size(axis)
        ends = count - 1
        head = lax.slice_in_dim(cells, 0, width, axis=dim)
        tail = lax.slice_in_dim(cells, cells.shape[dim] - width, cells.shape[dim], axis=dim)
        cells = jnp.concatenate(
            [
                lax.ppermute(tail, axis, [(i, (i + 1) % count) for i in range(ends)]),
                cells,
                lax.ppermute(head, axis, [((i + 1) % count, i) for i in range(ends)]),
            ],
            axis=dim,
        )
    return cells


def body(
    state,
    tile_ids,
    kernel_one,
    bias_one,
    kernel_two,
    bias_two,
    kernel_three,
    bias_three,
    kernel_flux,
    bias_flux,
):
    moments, block_h, block_w = state.shape
    col_count = lax.axis_size("col")
    row_count = lax.axis_size("row")
    my_row = lax.axis_index("row")
    my_col = lax.axis_index("col")
    margin = sum(dilations) + 1
    per_row = block_h // TILE
    per_col = block_w // TILE
    per_block = per_row * per_col
    grid_h = block_h * row_count
    grid_w = block_w * col_count
    layers = (
        (kernel_one, bias_one),
        (kernel_two, bias_two),
        (kernel_three, bias_three),
        (kernel_flux, bias_flux),
    )
    listed = tile_ids[0]
    mine = (listed // per_block) == my_col
    local_ids = listed % per_block
    chosen = jnp.any(
        mine[None, :] & (local_ids[None, :] == jnp.arange(per_block, dtype=jnp.int32)[:, None]), axis=1
    )
    own_mask = jnp.broadcast_to(
        chosen.reshape(per_row, 1, per_col, 1), (per_row, TILE, per_col, TILE)
    ).reshape(1, block_h, block_w)
    spare = jnp.zeros((16 - moments - 1, block_h, block_w), state.dtype)
    marked = jnp.concatenate([state, own_mask.astype(state.dtype), spare], axis=0).transpose(1, 0, 2)
    rows_done = with_halo(marked, (("row", 0),), margin)
    ext_h = rows_done.shape[0]
    ext_w = block_w + 2 * margin
    ends = col_count - 1
    x = jnp.concatenate(
        [
            lax.ppermute(rows_done[:, :, -margin:], "col", [(i, i + 1) for i in range(ends)]),
            rows_done,
            lax.ppermute(rows_done[:, :, :margin], "col", [(i + 1, i) for i in range(ends)]),
            jnp.zeros((ext_h, 16, LANES - ext_w), state.dtype),
        ],
        axis=2,
    )
    lims = []
    offset = margin
    out_h, out_w = ext_h, ext_w
    for spread in dilations:
        offset = offset - spread
        out_h, out_w = out_h - 2 * spread, out_w - 2 * spread
        top = offset - my_row * block_h
        left = offset - my_col * block_w
        lims += [
            jnp.maximum(top, 0),
            jnp.minimum(out_h, grid_h + top),
            jnp.maximum(left, 0),
            jnp.minimum(out_w, grid_w + left),
        ]
    lims = jnp.stack(lims).astype(jnp.int32)

    flux = run_net(x, lims, layers, LANES, 32)[:, : 2 * moments, : block_w + 2].transpose(1, 0, 2)
    cell_mask = x[margin - 1 : margin + block_h + 1, moments, margin - 1 : margin + block_w + 1] > 0
    rimmed = jnp.where(cell_mask[None], flux, jnp.zeros((), jnp.bfloat16))
    across = rimmed[:moments, 1:-1, :].astype(jnp.float32)
    downward = rimmed[moments:, :, 1:-1].astype(jnp.float32)
    difference = across[:, :, 2:] - across[:, :, :-2] + (downward[:, 2:, :] - downward[:, :-2, :])
    return (-0.5 * difference).astype(jnp.bfloat16)


def solution(mesh):
    return jax.shard_map(
        body,
        mesh=mesh,
        in_specs=(P(None, "row", "col"), P("row", None), P(), P(), P(), P(), P(), P(), P(), P()),
        out_specs=P(None, "row", "col"),
        check_vma=False,
    )
```

```python
import jax
import jax.numpy as jnp
from jax import lax
from jax.experimental import pallas as pl
from jax.experimental.pallas import tpu as pltpu
from jax.sharding import PartitionSpec as P

TILE = 64


dilations = (1, 2, 4, 8)
LANES = 384


def _net_kernel(lim_ref, x_ref, k1, b1, k2, b2, k3, b3, kf, bfl, out_ref, buf_a, buf_b):
    lanes = lax.broadcasted_iota(jnp.int32, (1, LANES), 1)

    def layer(src, dst, n_rows, spread, kmat, bias, index, last):
        kv = kmat[...]
        bv = bias[...]
        if not last:
            after = dilations[index + 1]
            row_lo = lim_ref[4 * index]
            row_hi = lim_ref[4 * index + 1]
            col_ok = (lanes >= lim_ref[4 * index + 2]) & (lanes < lim_ref[4 * index + 3])

        def row(y, carry):
            pieces = []
            for a in range(3):
                line = src[y + spread * a]
                if index == 0:
                    for e in range(3):
                        pieces.append(line if e == 0 else pltpu.roll(line, LANES - spread * e, 1))
                else:
                    pieces.append(line)
            col = jnp.concatenate(pieces, axis=0)
            acc = jnp.dot(kv, col, preferred_element_type=jnp.float32) + bv
            if last:
                dst[y] = acc[:, : dst.shape[2]].astype(dst.dtype)
            else:
                half = 0.5 * acc
                act = half + half * jnp.tanh(half)
                keep = col_ok & (y >= row_lo) & (y < row_hi)
                kept = jnp.where(keep, act, 0.0).astype(dst.dtype)
                dst[y] = jnp.concatenate(
                    [kept] + [pltpu.roll(kept, LANES - after * e, 1) for e in (1, 2)], axis=0
                )
            return carry

        lax.fori_loop(0, n_rows, row, 0, unroll=(8, 14, 16, 16)[index])

    h0 = x_ref.shape[0]
    h1 = h0 - 2
    h2 = h1 - 4
    h3 = h2 - 8
    h4 = h3 - 16
    layer(x_ref, buf_a, h1, 1, k1, b1, 0, False)
    layer(buf_a, buf_b, h2, 2, k2, b2, 1, False)
    layer(buf_b, buf_a, h3, 4, k3, b3, 2, False)
    layer(buf_a, out_ref, h4, 8, kf, bfl, 3, True)


def _kmat(kernel, cin):
    o, c = kernel.shape[:2]
    k = jnp.pad(kernel, ((0, 0), (0, cin - c), (0, 0), (0, 0)))
    return k.transpose(0, 2, 3, 1).reshape(o, 9 * cin)


def run_net(x, lims, layers, out_w, out_ch):
    (k1, b1), (k2, b2), (k3, b3), (kf, bf) = layers
    hid = k1.shape[0]
    h0 = x.shape[0]
    kf_p = jnp.pad(kf, ((0, out_ch - kf.shape[0]), (0, 0), (0, 0), (0, 0)))
    bf_p = jnp.pad(bf, (0, out_ch - bf.shape[0]))
    args = (
        lims, x,
        _kmat(k1, x.shape[1]), b1.reshape(-1, 1),
        _kmat(k2, hid), b2.reshape(-1, 1),
        _kmat(k3, hid), b3.reshape(-1, 1),
        _kmat(kf_p, hid), bf_p.reshape(-1, 1),
    )
    vspec = pl.BlockSpec(memory_space=pltpu.VMEM)
    return pl.pallas_call(
        _net_kernel,
        out_shape=jax.ShapeDtypeStruct((h0 - 30, out_ch, out_w), jnp.bfloat16),
        in_specs=[pl.BlockSpec(memory_space=pltpu.SMEM)] + [vspec] * 9,
        out_specs=vspec,
        scratch_shapes=[
            pltpu.VMEM((h0 - 2, 3 * hid, LANES), jnp.bfloat16),
            pltpu.VMEM((h0 - 6, 3 * hid, LANES), jnp.bfloat16),
        ],
        compiler_params=pltpu.CompilerParams(vmem_limit_bytes=60 * 1024 * 1024),
    )(*args)


def with_halo(cells, sides, width):
    for axis, dim in sides:
        count = lax.axis_size(axis)
        ends = count - 1
        head = lax.slice_in_dim(cells, 0, width, axis=dim)
        tail = lax.slice_in_dim(cells, cells.shape[dim] - width, cells.shape[dim], axis=dim)
        cells = jnp.concatenate(
            [
                lax.ppermute(tail, axis, [(i, (i + 1) % count) for i in range(ends)]),
                cells,
                lax.ppermute(head, axis, [((i + 1) % count, i) for i in range(ends)]),
            ],
            axis=dim,
        )
    return cells


def body(
    state,
    tile_ids,
    kernel_one,
    bias_one,
    kernel_two,
    bias_two,
    kernel_three,
    bias_three,
    kernel_flux,
    bias_flux,
):
    moments, block_h, block_w = state.shape
    col_count = lax.axis_size("col")
    row_count = lax.axis_size("row")
    my_row = lax.axis_index("row")
    my_col = lax.axis_index("col")
    margin = sum(dilations) + 1
    per_row = block_h // TILE
    per_col = block_w // TILE
    per_block = per_row * per_col
    grid_h = block_h * row_count
    grid_w = block_w * col_count
    layers = (
        (kernel_one, bias_one),
        (kernel_two, bias_two),
        (kernel_three, bias_three),
        (kernel_flux, bias_flux),
    )
    listed = tile_ids[0]
    mine = (listed // per_block) == my_col
    local_ids = listed % per_block
    chosen = jnp.any(
        mine[None, :] & (local_ids[None, :] == jnp.arange(per_block, dtype=jnp.int32)[:, None]), axis=1
    )
    own_mask = jnp.broadcast_to(
        chosen.reshape(per_row, 1, per_col, 1), (per_row, TILE, per_col, TILE)
    ).reshape(1, block_h, block_w)
    spare = jnp.zeros((16 - moments - 1, block_h, block_w), state.dtype)
    marked = jnp.concatenate([state, own_mask.astype(state.dtype), spare], axis=0).transpose(1, 0, 2)
    rows_done = with_halo(marked, (("row", 0),), margin)
    ext_h = rows_done.shape[0]
    ext_w = block_w + 2 * margin
    ends = col_count - 1
    x = jnp.concatenate(
        [
            lax.ppermute(rows_done[:, :, -margin:], "col", [(i, i + 1) for i in range(ends)]),
            rows_done,
            lax.ppermute(rows_done[:, :, :margin], "col", [(i + 1, i) for i in range(ends)]),
            jnp.zeros((ext_h, 16, LANES - ext_w), state.dtype),
        ],
        axis=2,
    )
    lims = []
    offset = margin
    out_h, out_w = ext_h, ext_w
    for spread in dilations:
        offset = offset - spread
        out_h, out_w = out_h - 2 * spread, out_w - 2 * spread
        top = offset - my_row * block_h
        left = offset - my_col * block_w
        lims += [
            jnp.maximum(top, 0),
            jnp.minimum(out_h, grid_h + top),
            jnp.maximum(left, 0),
            jnp.minimum(out_w, grid_w + left),
        ]
    lims = jnp.stack(lims).astype(jnp.int32)

    flux = run_net(x, lims, layers, LANES, 32)[:, : 2 * moments, : block_w + 2].transpose(1, 0, 2)
    cell_mask = x[margin - 1 : margin + block_h + 1, moments, margin - 1 : margin + block_w + 1] > 0
    rimmed = jnp.where(cell_mask[None], flux, jnp.zeros((), jnp.bfloat16))
    across = rimmed[:moments, 1:-1, :].astype(jnp.float32)
    downward = rimmed[moments:, :, 1:-1].astype(jnp.float32)
    difference = across[:, :, 2:] - across[:, :, :-2] + (downward[:, 2:, :] - downward[:, :-2, :])
    return (-0.5 * difference).astype(jnp.bfloat16)


def solution(mesh):
    return jax.shard_map(
        body,
        mesh=mesh,
        in_specs=(P(None, "row", "col"), P("row", None), P(), P(), P(), P(), P(), P(), P(), P()),
        out_specs=P(None, "row", "col"),
        check_vma=False,
    )
```

```python
import jax
import jax.numpy as jnp
from jax import lax
from jax.experimental import pallas as pl
from jax.experimental.pallas import tpu as pltpu
from jax.sharding import PartitionSpec as P

TILE = 64


dilations = (1, 2, 4, 8)
LANES = 384


def _net_kernel(lim_ref, x_ref, k1, b1, k2, b2, k3, b3, kf, bfl, out_ref, buf_a, buf_b):
    lanes = lax.broadcasted_iota(jnp.int32, (1, LANES), 1)

    def layer(src, dst, n_rows, spread, kmat, bias, index, last):
        kv = kmat[...]
        bv = bias[...]
        if not last:
            after = dilations[index + 1]
            row_lo = lim_ref[4 * index]
            row_hi = lim_ref[4 * index + 1]
            col_ok = (lanes >= lim_ref[4 * index + 2]) & (lanes < lim_ref[4 * index + 3])

        def row(y, carry):
            pieces = []
            for a in range(3):
                line = src[y + spread * a]
                if index == 0:
                    for e in range(3):
                        pieces.append(line if e == 0 else pltpu.roll(line, LANES - spread * e, 1))
                else:
                    pieces.append(line)
            col = jnp.concatenate(pieces, axis=0)
            acc = jnp.dot(kv, col, preferred_element_type=jnp.float32) + bv
            if last:
                dst[y] = acc[:, : dst.shape[2]].astype(dst.dtype)
            else:
                half = 0.5 * acc
                act = half + half * jnp.tanh(half)
                keep = col_ok & (y >= row_lo) & (y < row_hi)
                kept = jnp.where(keep, act, 0.0).astype(dst.dtype)
                dst[y] = jnp.concatenate(
                    [kept] + [pltpu.roll(kept, LANES - after * e, 1) for e in (1, 2)], axis=0
                )
            return carry

        lax.fori_loop(0, n_rows, row, 0, unroll=(8, 14, 16, 16)[index])

    h0 = x_ref.shape[0]
    h1 = h0 - 2
    h2 = h1 - 4
    h3 = h2 - 8
    h4 = h3 - 16
    layer(x_ref, buf_a, h1, 1, k1, b1, 0, False)
    layer(buf_a, buf_b, h2, 2, k2, b2, 1, False)
    layer(buf_b, buf_a, h3, 4, k3, b3, 2, False)
    layer(buf_a, out_ref, h4, 8, kf, bfl, 3, True)


def _kmat(kernel, cin):
    o, c = kernel.shape[:2]
    k = jnp.pad(kernel, ((0, 0), (0, cin - c), (0, 0), (0, 0)))
    return k.transpose(0, 2, 3, 1).reshape(o, 9 * cin)


def run_net(x, lims, layers, out_w, out_ch):
    (k1, b1), (k2, b2), (k3, b3), (kf, bf) = layers
    hid = k1.shape[0]
    h0 = x.shape[0]
    kf_p = jnp.pad(kf, ((0, out_ch - kf.shape[0]), (0, 0), (0, 0), (0, 0)))
    bf_p = jnp.pad(bf, (0, out_ch - bf.shape[0]))
    args = (
        lims, x,
        _kmat(k1, x.shape[1]), b1.reshape(-1, 1),
        _kmat(k2, hid), b2.reshape(-1, 1),
        _kmat(k3, hid), b3.reshape(-1, 1),
        _kmat(kf_p, hid), bf_p.reshape(-1, 1),
    )
    vspec = pl.BlockSpec(memory_space=pltpu.VMEM)
    return pl.pallas_call(
        _net_kernel,
        out_shape=jax.ShapeDtypeStruct((h0 - 30, out_ch, out_w), jnp.bfloat16),
        in_specs=[pl.BlockSpec(memory_space=pltpu.SMEM)] + [vspec] * 9,
        out_specs=vspec,
        scratch_shapes=[
            pltpu.VMEM((h0 - 2, 3 * hid, LANES), jnp.bfloat16),
            pltpu.VMEM((h0 - 6, 3 * hid, LANES), jnp.bfloat16),
        ],
        compiler_params=pltpu.CompilerParams(vmem_limit_bytes=60 * 1024 * 1024),
    )(*args)


def with_halo(cells, sides, width):
    for axis, dim in sides:
        count = lax.axis_size(axis)
        ends = count - 1
        head = lax.slice_in_dim(cells, 0, width, axis=dim)
        tail = lax.slice_in_dim(cells, cells.shape[dim] - width, cells.shape[dim], axis=dim)
        cells = jnp.concatenate(
            [
                lax.ppermute(tail, axis, [(i, (i + 1) % count) for i in range(ends)]),
                cells,
                lax.ppermute(head, axis, [((i + 1) % count, i) for i in range(ends)]),
            ],
            axis=dim,
        )
    return cells


def body(
    state,
    tile_ids,
    kernel_one,
    bias_one,
    kernel_two,
    bias_two,
    kernel_three,
    bias_three,
    kernel_flux,
    bias_flux,
):
    moments, block_h, block_w = state.shape
    col_count = lax.axis_size("col")
    row_count = lax.axis_size("row")
    my_row = lax.axis_index("row")
    my_col = lax.axis_index("col")
    margin = sum(dilations) + 1
    per_row = block_h // TILE
    per_col = block_w // TILE
    per_block = per_row * per_col
    grid_h = block_h * row_count
    grid_w = block_w * col_count
    layers = (
        (kernel_one, bias_one),
        (kernel_two, bias_two),
        (kernel_three, bias_three),
        (kernel_flux, bias_flux),
    )
    listed = tile_ids[0]
    mine = (listed // per_block) == my_col
    local_ids = listed % per_block
    chosen = jnp.any(
        mine[None, :] & (local_ids[None, :] == jnp.arange(per_block, dtype=jnp.int32)[:, None]), axis=1
    )
    own_mask = jnp.broadcast_to(
        chosen.reshape(per_row, 1, per_col, 1), (per_row, TILE, per_col, TILE)
    ).reshape(1, block_h, block_w)
    spare = jnp.zeros((16 - moments - 1, block_h, block_w), state.dtype)
    marked = jnp.concatenate([state, own_mask.astype(state.dtype), spare], axis=0)
    rows_done = jnp.concatenate(
        [
            lax.ppermute(marked[:, -margin:], "row", [(i, i + 1) for i in range(row_count - 1)]),
            marked,
            lax.ppermute(marked[:, :margin], "row", [(i + 1, i) for i in range(row_count - 1)]),
        ],
        axis=1,
    ).transpose(1, 0, 2)
    ext_h = rows_done.shape[0]
    ext_w = block_w + 2 * margin
    ends = col_count - 1
    x = jnp.concatenate(
        [
            lax.ppermute(rows_done[:, :, -margin:], "col", [(i, i + 1) for i in range(ends)]),
            rows_done,
            lax.ppermute(rows_done[:, :, :margin], "col", [(i + 1, i) for i in range(ends)]),
            jnp.zeros((ext_h, 16, LANES - ext_w), state.dtype),
        ],
        axis=2,
    )
    lims = []
    offset = margin
    out_h, out_w = ext_h, ext_w
    for spread in dilations:
        offset = offset - spread
        out_h, out_w = out_h - 2 * spread, out_w - 2 * spread
        top = offset - my_row * block_h
        left = offset - my_col * block_w
        lims += [
            jnp.maximum(top, 0),
            jnp.minimum(out_h, grid_h + top),
            jnp.maximum(left, 0),
            jnp.minimum(out_w, grid_w + left),
        ]
    lims = jnp.stack(lims).astype(jnp.int32)

    flux = run_net(x, lims, layers, LANES, 32)[:, : 2 * moments, : block_w + 2].transpose(1, 0, 2)
    cell_mask = x[margin - 1 : margin + block_h + 1, moments, margin - 1 : margin + block_w + 1] > 0
    rimmed = jnp.where(cell_mask[None], flux, jnp.zeros((), jnp.bfloat16))
    across = rimmed[:moments, 1:-1, :].astype(jnp.float32)
    downward = rimmed[moments:, :, 1:-1].astype(jnp.float32)
    difference = across[:, :, 2:] - across[:, :, :-2] + (downward[:, 2:, :] - downward[:, :-2, :])
    return (-0.5 * difference).astype(jnp.bfloat16)


def solution(mesh):
    return jax.shard_map(
        body,
        mesh=mesh,
        in_specs=(P(None, "row", "col"), P("row", None), P(), P(), P(), P(), P(), P(), P(), P()),
        out_specs=P(None, "row", "col"),
        check_vma=False,
    )
```

```python
import jax
import jax.numpy as jnp
from jax import lax
from jax.experimental import pallas as pl
from jax.experimental.pallas import tpu as pltpu
from jax.sharding import PartitionSpec as P

TILE = 64


dilations = (1, 2, 4, 8)
LANES = 384


def _net_kernel(lim_ref, x_ref, k1, b1, k2, b2, k3, b3, kf, bfl, out_ref, buf_a, buf_b):
    lanes = lax.broadcasted_iota(jnp.int32, (1, LANES), 1)

    def layer(src, dst, n_rows, spread, kmat, bias, index, last):
        kv = kmat[...]
        bv = bias[...]
        if not last:
            after = dilations[index + 1]
            row_lo = lim_ref[4 * index]
            row_hi = lim_ref[4 * index + 1]
            col_ok = (lanes >= lim_ref[4 * index + 2]) & (lanes < lim_ref[4 * index + 3])

        def row(y, carry):
            pieces = []
            for a in range(3):
                line = src[y + spread * a]
                if index == 0:
                    for e in range(3):
                        pieces.append(line if e == 0 else pltpu.roll(line, LANES - spread * e, 1))
                else:
                    pieces.append(line)
            col = jnp.concatenate(pieces, axis=0)
            acc = jnp.dot(kv, col, preferred_element_type=jnp.float32) + bv
            if last:
                dst[y] = acc[:, : dst.shape[2]].astype(dst.dtype)
            else:
                half = 0.5 * acc
                act = half + half * jnp.tanh(half)
                keep = col_ok & (y >= row_lo) & (y < row_hi)
                kept = jnp.where(keep, act, 0.0).astype(dst.dtype)
                dst[y] = jnp.concatenate(
                    [kept] + [pltpu.roll(kept, LANES - after * e, 1) for e in (1, 2)], axis=0
                )
            return carry

        lax.fori_loop(0, n_rows, row, 0, unroll=(8, 14, 16, 16)[index])

    h0 = x_ref.shape[0]
    h1 = h0 - 2
    h2 = h1 - 4
    h3 = h2 - 8
    h4 = h3 - 16
    layer(x_ref, buf_a, h1, 1, k1, b1, 0, False)
    layer(buf_a, buf_b, h2, 2, k2, b2, 1, False)
    layer(buf_b, buf_a, h3, 4, k3, b3, 2, False)
    layer(buf_a, out_ref, h4, 8, kf, bfl, 3, True)


def _kmat(kernel, cin):
    o, c = kernel.shape[:2]
    k = jnp.pad(kernel, ((0, 0), (0, cin - c), (0, 0), (0, 0)))
    return k.transpose(0, 2, 3, 1).reshape(o, 9 * cin)


def run_net(x, lims, layers, out_w, out_ch):
    (k1, b1), (k2, b2), (k3, b3), (kf, bf) = layers
    hid = k1.shape[0]
    h0 = x.shape[0]
    kf_p = jnp.pad(kf, ((0, out_ch - kf.shape[0]), (0, 0), (0, 0), (0, 0)))
    bf_p = jnp.pad(bf, (0, out_ch - bf.shape[0]))
    args = (
        lims, x,
        _kmat(k1, x.shape[1]), b1.reshape(-1, 1),
        _kmat(k2, hid), b2.reshape(-1, 1),
        _kmat(k3, hid), b3.reshape(-1, 1),
        _kmat(kf_p, hid), bf_p.reshape(-1, 1),
    )
    vspec = pl.BlockSpec(memory_space=pltpu.VMEM)
    return pl.pallas_call(
        _net_kernel,
        out_shape=jax.ShapeDtypeStruct((h0 - 30, out_ch, out_w), jnp.bfloat16),
        in_specs=[pl.BlockSpec(memory_space=pltpu.SMEM)] + [vspec] * 9,
        out_specs=vspec,
        scratch_shapes=[
            pltpu.VMEM((h0 - 2, 3 * hid, LANES), jnp.bfloat16),
            pltpu.VMEM((h0 - 6, 3 * hid, LANES), jnp.bfloat16),
        ],
        compiler_params=pltpu.CompilerParams(vmem_limit_bytes=60 * 1024 * 1024),
    )(*args)


def with_halo(cells, sides, width):
    for axis, dim in sides:
        count = lax.axis_size(axis)
        ends = count - 1
        head = lax.slice_in_dim(cells, 0, width, axis=dim)
        tail = lax.slice_in_dim(cells, cells.shape[dim] - width, cells.shape[dim], axis=dim)
        cells = jnp.concatenate(
            [
                lax.ppermute(tail, axis, [(i, (i + 1) % count) for i in range(ends)]),
                cells,
                lax.ppermute(head, axis, [((i + 1) % count, i) for i in range(ends)]),
            ],
            axis=dim,
        )
    return cells


def body(
    state,
    tile_ids,
    kernel_one,
    bias_one,
    kernel_two,
    bias_two,
    kernel_three,
    bias_three,
    kernel_flux,
    bias_flux,
):
    moments, block_h, block_w = state.shape
    col_count = lax.axis_size("col")
    row_count = lax.axis_size("row")
    my_row = lax.axis_index("row")
    my_col = lax.axis_index("col")
    margin = sum(dilations) + 1
    per_row = block_h // TILE
    per_col = block_w // TILE
    per_block = per_row * per_col
    grid_h = block_h * row_count
    grid_w = block_w * col_count
    layers = (
        (kernel_one, bias_one),
        (kernel_two, bias_two),
        (kernel_three, bias_three),
        (kernel_flux, bias_flux),
    )
    listed = tile_ids[0]
    mine = (listed // per_block) == my_col
    local_ids = listed % per_block
    chosen = jnp.any(
        mine[None, :] & (local_ids[None, :] == jnp.arange(per_block, dtype=jnp.int32)[:, None]), axis=1
    )
    own_mask = jnp.broadcast_to(
        chosen.reshape(per_row, 1, per_col, 1), (per_row, TILE, per_col, TILE)
    ).reshape(1, block_h, block_w)
    spare = jnp.zeros((16 - moments - 1, block_h, block_w), state.dtype)
    marked = jnp.concatenate([state, own_mask.astype(state.dtype), spare], axis=0)
    turned = marked.transpose(1, 0, 2)
    downs = [(i, i + 1) for i in range(row_count - 1)]
    ups = [(i + 1, i) for i in range(row_count - 1)]
    ends = col_count - 1
    from_above = lax.ppermute(marked[:, -margin:], "row", downs).transpose(1, 0, 2)
    from_below = lax.ppermute(marked[:, :margin], "row", ups).transpose(1, 0, 2)
    sides = jnp.concatenate(
        [
            lax.ppermute(turned[:, :, -margin:], "col", [(i, i + 1) for i in range(ends)]),
            lax.ppermute(turned[:, :, :margin], "col", [(i + 1, i) for i in range(ends)]),
        ],
        axis=2,
    )
    side_rows = jnp.concatenate(
        [lax.ppermute(sides[-margin:], "row", downs), sides, lax.ppermute(sides[:margin], "row", ups)],
        axis=0,
    )
    ext_h = block_h + 2 * margin
    ext_w = block_w + 2 * margin
    x = jnp.concatenate(
        [
            side_rows[:, :, :margin],
            jnp.concatenate([from_above, turned, from_below], axis=0),
            side_rows[:, :, margin:],
            jnp.zeros((ext_h, 16, LANES - ext_w), state.dtype),
        ],
        axis=2,
    )
    lims = []
    offset = margin
    out_h, out_w = ext_h, ext_w
    for spread in dilations:
        offset = offset - spread
        out_h, out_w = out_h - 2 * spread, out_w - 2 * spread
        top = offset - my_row * block_h
        left = offset - my_col * block_w
        lims += [
            jnp.maximum(top, 0),
            jnp.minimum(out_h, grid_h + top),
            jnp.maximum(left, 0),
            jnp.minimum(out_w, grid_w + left),
        ]
    lims = jnp.stack(lims).astype(jnp.int32)

    flux = run_net(x, lims, layers, LANES, 32)[:, : 2 * moments, : block_w + 2].transpose(1, 0, 2)
    cell_mask = x[margin - 1 : margin + block_h + 1, moments, margin - 1 : margin + block_w + 1] > 0
    rimmed = jnp.where(cell_mask[None], flux, jnp.zeros((), jnp.bfloat16))
    across = rimmed[:moments, 1:-1, :].astype(jnp.float32)
    downward = rimmed[moments:, :, 1:-1].astype(jnp.float32)
    difference = across[:, :, 2:] - across[:, :, :-2] + (downward[:, 2:, :] - downward[:, :-2, :])
    return (-0.5 * difference).astype(jnp.bfloat16)


def solution(mesh):
    return jax.shard_map(
        body,
        mesh=mesh,
        in_specs=(P(None, "row", "col"), P("row", None), P(), P(), P(), P(), P(), P(), P(), P()),
        out_specs=P(None, "row", "col"),
        check_vma=False,
    )
```

```python
import jax
import jax.numpy as jnp
from jax import lax
from jax.experimental import pallas as pl
from jax.experimental.pallas import tpu as pltpu
from jax.sharding import PartitionSpec as P

TILE = 64


dilations = (1, 2, 4, 8)
LANES = 384


def _net_kernel(lim_ref, x_ref, k1, b1, k2, b2, k3, b3, kf, bfl, out_ref, buf_a, buf_b):
    lanes = lax.broadcasted_iota(jnp.int32, (1, LANES), 1)

    def layer(src, dst, n_rows, spread, kmat, bias, index, last):
        kv = kmat[...]
        bv = bias[...]
        if not last:
            after = dilations[index + 1]
            row_lo = lim_ref[4 * index]
            row_hi = lim_ref[4 * index + 1]
            col_ok = (lanes >= lim_ref[4 * index + 2]) & (lanes < lim_ref[4 * index + 3])

        def row(y, carry):
            pieces = []
            for a in range(3):
                line = src[y + spread * a]
                if index == 0:
                    for e in range(3):
                        pieces.append(line if e == 0 else pltpu.roll(line, LANES - spread * e, 1))
                else:
                    pieces.append(line)
            col = jnp.concatenate(pieces, axis=0)
            acc = jnp.dot(kv, col, preferred_element_type=jnp.float32) + bv
            if last:
                dst[y] = acc[:, : dst.shape[2]].astype(dst.dtype)
            else:
                half = 0.5 * acc
                act = half + half * jnp.tanh(half)
                keep = col_ok & (y >= row_lo) & (y < row_hi)
                kept = jnp.where(keep, act, 0.0).astype(dst.dtype)
                dst[y] = jnp.concatenate(
                    [kept] + [pltpu.roll(kept, LANES - after * e, 1) for e in (1, 2)], axis=0
                )
            return carry

        lax.fori_loop(0, n_rows, row, 0, unroll=(8, 14, 16, 16)[index])

    h0 = x_ref.shape[0]
    h1 = h0 - 2
    h2 = h1 - 4
    h3 = h2 - 8
    h4 = h3 - 16
    layer(x_ref, buf_a, h1, 1, k1, b1, 0, False)
    layer(buf_a, buf_b, h2, 2, k2, b2, 1, False)
    layer(buf_b, buf_a, h3, 4, k3, b3, 2, False)
    layer(buf_a, out_ref, h4, 8, kf, bfl, 3, True)


def _kmat(kernel, cin):
    o, c = kernel.shape[:2]
    k = jnp.pad(kernel, ((0, 0), (0, cin - c), (0, 0), (0, 0)))
    return k.transpose(0, 2, 3, 1).reshape(o, 9 * cin)


def run_net(x, lims, layers, out_w, out_ch):
    (k1, b1), (k2, b2), (k3, b3), (kf, bf) = layers
    hid = k1.shape[0]
    h0 = x.shape[0]
    kf_p = jnp.pad(kf, ((0, out_ch - kf.shape[0]), (0, 0), (0, 0), (0, 0)))
    bf_p = jnp.pad(bf, (0, out_ch - bf.shape[0]))
    args = (
        lims, x,
        _kmat(k1, x.shape[1]), b1.reshape(-1, 1),
        _kmat(k2, hid), b2.reshape(-1, 1),
        _kmat(k3, hid), b3.reshape(-1, 1),
        _kmat(kf_p, hid), bf_p.reshape(-1, 1),
    )
    vspec = pl.BlockSpec(memory_space=pltpu.VMEM)
    return pl.pallas_call(
        _net_kernel,
        out_shape=jax.ShapeDtypeStruct((h0 - 30, out_ch, out_w), jnp.bfloat16),
        in_specs=[pl.BlockSpec(memory_space=pltpu.SMEM)] + [vspec] * 9,
        out_specs=vspec,
        scratch_shapes=[
            pltpu.VMEM((h0 - 2, 3 * hid, LANES), jnp.bfloat16),
            pltpu.VMEM((h0 - 6, 3 * hid, LANES), jnp.bfloat16),
        ],
        compiler_params=pltpu.CompilerParams(vmem_limit_bytes=60 * 1024 * 1024),
    )(*args)


def with_halo(cells, sides, width):
    for axis, dim in sides:
        count = lax.axis_size(axis)
        ends = count - 1
        head = lax.slice_in_dim(cells, 0, width, axis=dim)
        tail = lax.slice_in_dim(cells, cells.shape[dim] - width, cells.shape[dim], axis=dim)
        cells = jnp.concatenate(
            [
                lax.ppermute(tail, axis, [(i, (i + 1) % count) for i in range(ends)]),
                cells,
                lax.ppermute(head, axis, [((i + 1) % count, i) for i in range(ends)]),
            ],
            axis=dim,
        )
    return cells


def body(
    state,
    tile_ids,
    kernel_one,
    bias_one,
    kernel_two,
    bias_two,
    kernel_three,
    bias_three,
    kernel_flux,
    bias_flux,
):
    moments, block_h, block_w = state.shape
    col_count = lax.axis_size("col")
    row_count = lax.axis_size("row")
    my_row = lax.axis_index("row")
    my_col = lax.axis_index("col")
    margin = sum(dilations) + 1
    per_row = block_h // TILE
    per_col = block_w // TILE
    per_block = per_row * per_col
    grid_h = block_h * row_count
    grid_w = block_w * col_count
    layers = (
        (kernel_one, bias_one),
        (kernel_two, bias_two),
        (kernel_three, bias_three),
        (kernel_flux, bias_flux),
    )
    listed = tile_ids[0]
    mine = (listed // per_block) == my_col
    local_ids = listed % per_block
    chosen = jnp.any(
        mine[None, :] & (local_ids[None, :] == jnp.arange(per_block, dtype=jnp.int32)[:, None]), axis=1
    )
    own_mask = jnp.broadcast_to(
        chosen.reshape(per_row, 1, per_col, 1), (per_row, TILE, per_col, TILE)
    ).reshape(1, block_h, block_w)
    spare = jnp.zeros((16 - moments - 1, block_h, block_w), state.dtype)
    marked = jnp.concatenate([state, own_mask.astype(state.dtype), spare], axis=0).transpose(1, 0, 2)
    ends = col_count - 1
    cols_done = jnp.concatenate(
        [
            lax.ppermute(marked[:, :, -margin:], "col", [(i, i + 1) for i in range(ends)]),
            marked,
            lax.ppermute(marked[:, :, :margin], "col", [(i + 1, i) for i in range(ends)]),
            jnp.zeros((block_h, 16, LANES - block_w - 2 * margin), state.dtype),
        ],
        axis=2,
    )
    x = jnp.concatenate(
        [
            lax.ppermute(cols_done[-margin:], "row", [(i, i + 1) for i in range(row_count - 1)]),
            cols_done,
            lax.ppermute(cols_done[:margin], "row", [(i + 1, i) for i in range(row_count - 1)]),
        ],
        axis=0,
    )
    ext_h = block_h + 2 * margin
    ext_w = block_w + 2 * margin
    lims = []
    offset = margin
    out_h, out_w = ext_h, ext_w
    for spread in dilations:
        offset = offset - spread
        out_h, out_w = out_h - 2 * spread, out_w - 2 * spread
        top = offset - my_row * block_h
        left = offset - my_col * block_w
        lims += [
            jnp.maximum(top, 0),
            jnp.minimum(out_h, grid_h + top),
            jnp.maximum(left, 0),
            jnp.minimum(out_w, grid_w + left),
        ]
    lims = jnp.stack(lims).astype(jnp.int32)

    flux = run_net(x, lims, layers, LANES, 32)[:, : 2 * moments, : block_w + 2].transpose(1, 0, 2)
    cell_mask = x[margin - 1 : margin + block_h + 1, moments, margin - 1 : margin + block_w + 1] > 0
    rimmed = jnp.where(cell_mask[None], flux, jnp.zeros((), jnp.bfloat16))
    across = rimmed[:moments, 1:-1, :].astype(jnp.float32)
    downward = rimmed[moments:, :, 1:-1].astype(jnp.float32)
    difference = across[:, :, 2:] - across[:, :, :-2] + (downward[:, 2:, :] - downward[:, :-2, :])
    return (-0.5 * difference).astype(jnp.bfloat16)


def solution(mesh):
    return jax.shard_map(
        body,
        mesh=mesh,
        in_specs=(P(None, "row", "col"), P("row", None), P(), P(), P(), P(), P(), P(), P(), P()),
        out_specs=P(None, "row", "col"),
        check_vma=False,
    )
```

```python
import jax
import jax.numpy as jnp
from jax import lax
from jax.experimental import pallas as pl
from jax.experimental.pallas import tpu as pltpu
from jax.sharding import PartitionSpec as P

TILE = 64


dilations = (1, 2, 4, 8)
LANES = 384


def _net_kernel(lim_ref, x_ref, k1, b1, k2, b2, k3, b3, kf, bfl, ring_ref, out_ref, buf_a, buf_b):
    lanes = lax.broadcasted_iota(jnp.int32, (1, LANES), 1)

    def layer(src, dst, n_rows, spread, kmat, bias, index, last):
        kv = kmat[...]
        bv = bias[...]
        if not last:
            after = dilations[index + 1]
            row_lo = lim_ref[4 * index]
            row_hi = lim_ref[4 * index + 1]
            col_ok = (lanes >= lim_ref[4 * index + 2]) & (lanes < lim_ref[4 * index + 3])

        def row(y, carry):
            pieces = []
            for a in range(3):
                line = src[y + spread * a]
                if index == 0:
                    for e in range(3):
                        pieces.append(line if e == 0 else pltpu.roll(line, LANES - spread * e, 1))
                else:
                    pieces.append(line)
            col = jnp.concatenate(pieces, axis=0)
            acc = jnp.dot(kv, col, preferred_element_type=jnp.float32) + bv
            if last:
                dst[y, : acc.shape[0]] = jnp.where(ring_ref[y] > 0, acc, 0.0).astype(dst.dtype)
            else:
                half = 0.5 * acc
                act = half + half * jnp.tanh(half)
                keep = col_ok & (y >= row_lo) & (y < row_hi)
                kept = jnp.where(keep, act, 0.0).astype(dst.dtype)
                dst[y] = jnp.concatenate(
                    [kept] + [pltpu.roll(kept, LANES - after * e, 1) for e in (1, 2)], axis=0
                )
            return carry

        lax.fori_loop(0, n_rows, row, 0, unroll=(8, 14, 16, 16)[index])

    h0 = x_ref.shape[0]
    h1 = h0 - 2
    h2 = h1 - 4
    h3 = h2 - 8
    h4 = h3 - 16
    layer(x_ref, buf_a, h1, 1, k1, b1, 0, False)
    layer(buf_a, buf_b, h2, 2, k2, b2, 1, False)
    layer(buf_b, buf_a, h3, 4, k3, b3, 2, False)
    layer(buf_a, buf_b, h4, 8, kf, bfl, 3, True)
    half_ch = kf.shape[0] // 2

    def close(y, carry):
        across = buf_b[y + 1, :half_ch].astype(jnp.float32)
        down = buf_b[y + 2, half_ch : 2 * half_ch].astype(jnp.float32) - buf_b[y, half_ch : 2 * half_ch].astype(jnp.float32)
        diff = (pltpu.roll(across, LANES - 2, 1) - across) + pltpu.roll(down, LANES - 1, 1)
        out_ref[y] = (-0.5 * diff)[: out_ref.shape[1], : out_ref.shape[2]].astype(out_ref.dtype)
        return carry

    lax.fori_loop(0, h4 - 2, close, 0, unroll=8)


def _kmat(kernel, cin):
    o, c = kernel.shape[:2]
    k = jnp.pad(kernel, ((0, 0), (0, cin - c), (0, 0), (0, 0)))
    return k.transpose(0, 2, 3, 1).reshape(o, 9 * cin)


def run_net(x, lims, ring, layers, out_w, out_ch):
    (k1, b1), (k2, b2), (k3, b3), (kf, bf) = layers
    hid = k1.shape[0]
    h0 = x.shape[0]
    moments = kf.shape[0] // 2
    gap = out_ch // 2 - moments
    kf_p = jnp.concatenate(
        [jnp.pad(part, ((0, gap), (0, 0), (0, 0), (0, 0))) for part in (kf[:moments], kf[moments:])], axis=0
    )
    bf_p = jnp.concatenate([jnp.pad(part, (0, gap)) for part in (bf[:moments], bf[moments:])])
    args = (
        lims, x,
        _kmat(k1, x.shape[1]), b1.reshape(-1, 1),
        _kmat(k2, hid), b2.reshape(-1, 1),
        _kmat(k3, hid), b3.reshape(-1, 1),
        _kmat(kf_p, hid), bf_p.reshape(-1, 1),
        ring,
    )
    vspec = pl.BlockSpec(memory_space=pltpu.VMEM)
    return pl.pallas_call(
        _net_kernel,
        out_shape=jax.ShapeDtypeStruct((h0 - 32, moments, out_w), jnp.bfloat16),
        in_specs=[pl.BlockSpec(memory_space=pltpu.SMEM)] + [vspec] * 10,
        out_specs=vspec,
        scratch_shapes=[
            pltpu.VMEM((h0 - 2, 3 * hid, LANES), jnp.bfloat16),
            pltpu.VMEM((h0 - 6, 3 * hid, LANES), jnp.bfloat16),
        ],
        compiler_params=pltpu.CompilerParams(vmem_limit_bytes=60 * 1024 * 1024),
    )(*args)


def with_halo(cells, sides, width):
    for axis, dim in sides:
        count = lax.axis_size(axis)
        ends = count - 1
        head = lax.slice_in_dim(cells, 0, width, axis=dim)
        tail = lax.slice_in_dim(cells, cells.shape[dim] - width, cells.shape[dim], axis=dim)
        cells = jnp.concatenate(
            [
                lax.ppermute(tail, axis, [(i, (i + 1) % count) for i in range(ends)]),
                cells,
                lax.ppermute(head, axis, [((i + 1) % count, i) for i in range(ends)]),
            ],
            axis=dim,
        )
    return cells


def body(
    state,
    tile_ids,
    kernel_one,
    bias_one,
    kernel_two,
    bias_two,
    kernel_three,
    bias_three,
    kernel_flux,
    bias_flux,
):
    moments, block_h, block_w = state.shape
    col_count = lax.axis_size("col")
    row_count = lax.axis_size("row")
    my_row = lax.axis_index("row")
    my_col = lax.axis_index("col")
    margin = sum(dilations) + 1
    per_row = block_h // TILE
    per_col = block_w // TILE
    per_block = per_row * per_col
    grid_h = block_h * row_count
    grid_w = block_w * col_count
    layers = (
        (kernel_one, bias_one),
        (kernel_two, bias_two),
        (kernel_three, bias_three),
        (kernel_flux, bias_flux),
    )
    listed = tile_ids[0]
    mine = (listed // per_block) == my_col
    local_ids = listed % per_block
    chosen = jnp.any(
        mine[None, :] & (local_ids[None, :] == jnp.arange(per_block, dtype=jnp.int32)[:, None]), axis=1
    )
    own_mask = jnp.broadcast_to(
        chosen.reshape(per_row, 1, per_col, 1), (per_row, TILE, per_col, TILE)
    ).reshape(1, block_h, block_w)
    spare = jnp.zeros((16 - moments - 1, block_h, block_w), state.dtype)
    marked = jnp.concatenate([state, own_mask.astype(state.dtype), spare], axis=0)
    rows_done = jnp.concatenate(
        [
            lax.ppermute(marked[:, -margin:], "row", [(i, i + 1) for i in range(row_count - 1)]),
            marked,
            lax.ppermute(marked[:, :margin], "row", [(i + 1, i) for i in range(row_count - 1)]),
        ],
        axis=1,
    ).transpose(1, 0, 2)
    ext_h = rows_done.shape[0]
    ext_w = block_w + 2 * margin
    ends = col_count - 1
    x = jnp.concatenate(
        [
            lax.ppermute(rows_done[:, :, -margin:], "col", [(i, i + 1) for i in range(ends)]),
            rows_done,
            lax.ppermute(rows_done[:, :, :margin], "col", [(i + 1, i) for i in range(ends)]),
            jnp.zeros((ext_h, 16, LANES - ext_w), state.dtype),
        ],
        axis=2,
    )
    lims = []
    offset = margin
    out_h, out_w = ext_h, ext_w
    for spread in dilations:
        offset = offset - spread
        out_h, out_w = out_h - 2 * spread, out_w - 2 * spread
        top = offset - my_row * block_h
        left = offset - my_col * block_w
        lims += [
            jnp.maximum(top, 0),
            jnp.minimum(out_h, grid_h + top),
            jnp.maximum(left, 0),
            jnp.minimum(out_w, grid_w + left),
        ]
    lims = jnp.stack(lims).astype(jnp.int32)

    ring = x[margin - 1 : margin + block_h + 1, moments : moments + 1, margin - 1 :].astype(jnp.float32)
    ring = jnp.pad(ring, ((0, 0), (0, 0), (0, LANES - ring.shape[2])))
    closure = run_net(x, lims, ring, layers, block_w, 32)
    return closure.transpose(1, 0, 2)


def solution(mesh):
    return jax.shard_map(
        body,
        mesh=mesh,
        in_specs=(P(None, "row", "col"), P("row", None), P(), P(), P(), P(), P(), P(), P(), P()),
        out_specs=P(None, "row", "col"),
        check_vma=False,
    )
```

```python
import jax
import jax.numpy as jnp
from jax import lax
from jax.experimental import pallas as pl
from jax.experimental.pallas import tpu as pltpu
from jax.sharding import PartitionSpec as P

TILE = 64


dilations = (1, 2, 4, 8)
LANES = 384


def _net_kernel(lim_ref, x_ref, k1, b1, k2, b2, k3, b3, kf, bfl, ring_ref, out_ref, buf_a, buf_b):
    lanes = lax.broadcasted_iota(jnp.int32, (1, LANES), 1)

    def layer(src, dst, n_rows, spread, kmat, bias, index, last):
        kv = kmat[...]
        bv = bias[...]
        if not last:
            after = dilations[index + 1]
            row_lo = lim_ref[4 * index]
            row_hi = lim_ref[4 * index + 1]
            col_ok = (lanes >= lim_ref[4 * index + 2]) & (lanes < lim_ref[4 * index + 3])

        def row(y, carry):
            pieces = []
            for a in range(3):
                line = src[y + spread * a]
                if index == 0:
                    for e in range(3):
                        pieces.append(line if e == 0 else pltpu.roll(line, LANES - spread * e, 1))
                else:
                    pieces.append(line)
            col = jnp.concatenate(pieces, axis=0)
            acc = jnp.dot(kv, col, preferred_element_type=jnp.float32) + bv
            if last:
                dst[y, : acc.shape[0]] = jnp.where(ring_ref[y] > 0, acc, 0.0).astype(dst.dtype)
            else:
                half = 0.5 * acc
                act = half + half * jnp.tanh(half)
                keep = col_ok & (y >= row_lo) & (y < row_hi)
                kept = jnp.where(keep, act, 0.0).astype(dst.dtype)
                dst[y] = jnp.concatenate(
                    [kept] + [pltpu.roll(kept, LANES - after * e, 1) for e in (1, 2)], axis=0
                )
            return carry

        lax.fori_loop(0, n_rows, row, 0, unroll=(8, 14, 16, 16)[index])

    h0 = x_ref.shape[0]
    h1 = h0 - 2
    h2 = h1 - 4
    h3 = h2 - 8
    h4 = h3 - 16
    layer(x_ref, buf_a, h1, 1, k1, b1, 0, False)
    layer(buf_a, buf_b, h2, 2, k2, b2, 1, False)
    layer(buf_b, buf_a, h3, 4, k3, b3, 2, False)
    layer(buf_a, buf_b, h4, 8, kf, bfl, 3, True)
    half_ch = kf.shape[0] // 2

    def close_row(y):
        across = buf_b[y + 1, :half_ch].astype(jnp.float32)
        down = buf_b[y + 2, half_ch : 2 * half_ch].astype(jnp.float32) - buf_b[y, half_ch : 2 * half_ch].astype(jnp.float32)
        diff = (pltpu.roll(across, LANES - 2, 1) - across) + pltpu.roll(down, LANES - 1, 1)
        return (-0.5 * diff)[: out_ref.shape[0], : out_ref.shape[2]]

    def close(t, carry):
        y = pl.multiple_of(16 * t, 16)
        group = jnp.stack([close_row(y + k) for k in range(16)], axis=1)
        out_ref[:, pl.ds(y, 16), :] = group.astype(out_ref.dtype)
        return carry

    lax.fori_loop(0, (h4 - 2) // 16, close, 0)


def _kmat(kernel, cin):
    o, c = kernel.shape[:2]
    k = jnp.pad(kernel, ((0, 0), (0, cin - c), (0, 0), (0, 0)))
    return k.transpose(0, 2, 3, 1).reshape(o, 9 * cin)


def run_net(x, lims, ring, layers, out_w, out_ch):
    (k1, b1), (k2, b2), (k3, b3), (kf, bf) = layers
    hid = k1.shape[0]
    h0 = x.shape[0]
    moments = kf.shape[0] // 2
    gap = out_ch // 2 - moments
    kf_p = jnp.concatenate(
        [jnp.pad(part, ((0, gap), (0, 0), (0, 0), (0, 0))) for part in (kf[:moments], kf[moments:])], axis=0
    )
    bf_p = jnp.concatenate([jnp.pad(part, (0, gap)) for part in (bf[:moments], bf[moments:])])
    args = (
        lims, x,
        _kmat(k1, x.shape[1]), b1.reshape(-1, 1),
        _kmat(k2, hid), b2.reshape(-1, 1),
        _kmat(k3, hid), b3.reshape(-1, 1),
        _kmat(kf_p, hid), bf_p.reshape(-1, 1),
        ring,
    )
    vspec = pl.BlockSpec(memory_space=pltpu.VMEM)
    return pl.pallas_call(
        _net_kernel,
        out_shape=jax.ShapeDtypeStruct((moments, h0 - 32, out_w), jnp.bfloat16),
        in_specs=[pl.BlockSpec(memory_space=pltpu.SMEM)] + [vspec] * 10,
        out_specs=vspec,
        scratch_shapes=[
            pltpu.VMEM((h0 - 2, 3 * hid, LANES), jnp.bfloat16),
            pltpu.VMEM((h0 - 6, 3 * hid, LANES), jnp.bfloat16),
        ],
        compiler_params=pltpu.CompilerParams(vmem_limit_bytes=60 * 1024 * 1024),
    )(*args)


def with_halo(cells, sides, width):
    for axis, dim in sides:
        count = lax.axis_size(axis)
        ends = count - 1
        head = lax.slice_in_dim(cells, 0, width, axis=dim)
        tail = lax.slice_in_dim(cells, cells.shape[dim] - width, cells.shape[dim], axis=dim)
        cells = jnp.concatenate(
            [
                lax.ppermute(tail, axis, [(i, (i + 1) % count) for i in range(ends)]),
                cells,
                lax.ppermute(head, axis, [((i + 1) % count, i) for i in range(ends)]),
            ],
            axis=dim,
        )
    return cells


def body(
    state,
    tile_ids,
    kernel_one,
    bias_one,
    kernel_two,
    bias_two,
    kernel_three,
    bias_three,
    kernel_flux,
    bias_flux,
):
    moments, block_h, block_w = state.shape
    col_count = lax.axis_size("col")
    row_count = lax.axis_size("row")
    my_row = lax.axis_index("row")
    my_col = lax.axis_index("col")
    margin = sum(dilations) + 1
    per_row = block_h // TILE
    per_col = block_w // TILE
    per_block = per_row * per_col
    grid_h = block_h * row_count
    grid_w = block_w * col_count
    layers = (
        (kernel_one, bias_one),
        (kernel_two, bias_two),
        (kernel_three, bias_three),
        (kernel_flux, bias_flux),
    )
    listed = tile_ids[0]
    mine = (listed // per_block) == my_col
    local_ids = listed % per_block
    chosen = jnp.any(
        mine[None, :] & (local_ids[None, :] == jnp.arange(per_block, dtype=jnp.int32)[:, None]), axis=1
    )
    own_mask = jnp.broadcast_to(
        chosen.reshape(per_row, 1, per_col, 1), (per_row, TILE, per_col, TILE)
    ).reshape(1, block_h, block_w)
    spare = jnp.zeros((16 - moments - 1, block_h, block_w), state.dtype)
    marked = jnp.concatenate([state, own_mask.astype(state.dtype), spare], axis=0)
    rows_done = jnp.concatenate(
        [
            lax.ppermute(marked[:, -margin:], "row", [(i, i + 1) for i in range(row_count - 1)]),
            marked,
            lax.ppermute(marked[:, :margin], "row", [(i + 1, i) for i in range(row_count - 1)]),
        ],
        axis=1,
    ).transpose(1, 0, 2)
    ext_h = rows_done.shape[0]
    ext_w = block_w + 2 * margin
    ends = col_count - 1
    x = jnp.concatenate(
        [
            lax.ppermute(rows_done[:, :, -margin:], "col", [(i, i + 1) for i in range(ends)]),
            rows_done,
            lax.ppermute(rows_done[:, :, :margin], "col", [(i + 1, i) for i in range(ends)]),
            jnp.zeros((ext_h, 16, LANES - ext_w), state.dtype),
        ],
        axis=2,
    )
    lims = []
    offset = margin
    out_h, out_w = ext_h, ext_w
    for spread in dilations:
        offset = offset - spread
        out_h, out_w = out_h - 2 * spread, out_w - 2 * spread
        top = offset - my_row * block_h
        left = offset - my_col * block_w
        lims += [
            jnp.maximum(top, 0),
            jnp.minimum(out_h, grid_h + top),
            jnp.maximum(left, 0),
            jnp.minimum(out_w, grid_w + left),
        ]
    lims = jnp.stack(lims).astype(jnp.int32)

    ring = x[margin - 1 : margin + block_h + 1, moments : moments + 1, margin - 1 :].astype(jnp.float32)
    ring = jnp.pad(ring, ((0, 0), (0, 0), (0, LANES - ring.shape[2])))
    closure = run_net(x, lims, ring, layers, block_w, 32)
    return closure


def solution(mesh):
    return jax.shard_map(
        body,
        mesh=mesh,
        in_specs=(P(None, "row", "col"), P("row", None), P(), P(), P(), P(), P(), P(), P(), P()),
        out_specs=P(None, "row", "col"),
        check_vma=False,
    )
```

```python
import functools
import jax
import jax.numpy as jnp
from jax import lax
from jax.experimental import pallas as pl
from jax.experimental.pallas import tpu as pltpu
from jax.sharding import PartitionSpec as P

TILE = 64


dilations = (1, 2, 4, 8)
LANES = 384


def _net_kernel(mark, lim_ref, x_ref, k1, b1, k2, b2, k3, b3, kf, bfl, out_ref, buf_a, buf_b):
    lanes = lax.broadcasted_iota(jnp.int32, (1, LANES), 1)

    def layer(src, dst, n_rows, spread, kmat, bias, index, last):
        kv = kmat[...]
        bv = bias[...]
        if not last:
            after = dilations[index + 1]
            row_lo = lim_ref[4 * index]
            row_hi = lim_ref[4 * index + 1]
            col_ok = (lanes >= lim_ref[4 * index + 2]) & (lanes < lim_ref[4 * index + 3])

        def row(y, carry):
            pieces = []
            for a in range(3):
                line = src[y + spread * a]
                if index == 0:
                    for e in range(3):
                        pieces.append(line if e == 0 else pltpu.roll(line, LANES - spread * e, 1))
                else:
                    pieces.append(line)
            col = jnp.concatenate(pieces, axis=0)
            acc = jnp.dot(kv, col, preferred_element_type=jnp.float32) + bv
            if last:
                reach = sum(dilations)
                flag = x_ref[y + reach].astype(jnp.float32)[mark : mark + 1]
                flag = pltpu.roll(flag, LANES - reach, 1)
                dst[y, : acc.shape[0]] = jnp.where(flag > 0, acc, 0.0).astype(dst.dtype)
            else:
                half = 0.5 * acc
                act = half + half * jnp.tanh(half)
                keep = col_ok & (y >= row_lo) & (y < row_hi)
                kept = jnp.where(keep, act, 0.0).astype(dst.dtype)
                dst[y] = jnp.concatenate(
                    [kept] + [pltpu.roll(kept, LANES - after * e, 1) for e in (1, 2)], axis=0
                )
            return carry

        lax.fori_loop(0, n_rows, row, 0, unroll=(8, 14, 16, 16)[index])

    h0 = x_ref.shape[0]
    h1 = h0 - 2
    h2 = h1 - 4
    h3 = h2 - 8
    h4 = h3 - 16
    layer(x_ref, buf_a, h1, 1, k1, b1, 0, False)
    layer(buf_a, buf_b, h2, 2, k2, b2, 1, False)
    layer(buf_b, buf_a, h3, 4, k3, b3, 2, False)
    layer(buf_a, buf_b, h4, 8, kf, bfl, 3, True)
    half_ch = kf.shape[0] // 2

    def close_row(y):
        across = buf_b[y + 1, :half_ch].astype(jnp.float32)
        down = buf_b[y + 2, half_ch : 2 * half_ch].astype(jnp.float32) - buf_b[y, half_ch : 2 * half_ch].astype(jnp.float32)
        diff = (pltpu.roll(across, LANES - 2, 1) - across) + pltpu.roll(down, LANES - 1, 1)
        return (-0.5 * diff)[: out_ref.shape[0], : out_ref.shape[2]]

    def close(t, carry):
        y = pl.multiple_of(16 * t, 16)
        group = jnp.stack([close_row(y + k) for k in range(16)], axis=1)
        out_ref[:, pl.ds(y, 16), :] = group.astype(out_ref.dtype)
        return carry

    lax.fori_loop(0, (h4 - 2) // 16, close, 0)


def _kmat(kernel, cin):
    o, c = kernel.shape[:2]
    k = jnp.pad(kernel, ((0, 0), (0, cin - c), (0, 0), (0, 0)))
    return k.transpose(0, 2, 3, 1).reshape(o, 9 * cin)


def run_net(x, lims, layers, out_w, out_ch):
    (k1, b1), (k2, b2), (k3, b3), (kf, bf) = layers
    hid = k1.shape[0]
    h0 = x.shape[0]
    moments = kf.shape[0] // 2
    gap = out_ch // 2 - moments
    kf_p = jnp.concatenate(
        [jnp.pad(part, ((0, gap), (0, 0), (0, 0), (0, 0))) for part in (kf[:moments], kf[moments:])], axis=0
    )
    bf_p = jnp.concatenate([jnp.pad(part, (0, gap)) for part in (bf[:moments], bf[moments:])])
    args = (
        lims, x,
        _kmat(k1, x.shape[1]), b1.reshape(-1, 1),
        _kmat(k2, hid), b2.reshape(-1, 1),
        _kmat(k3, hid), b3.reshape(-1, 1),
        _kmat(kf_p, hid), bf_p.reshape(-1, 1),
    )
    vspec = pl.BlockSpec(memory_space=pltpu.VMEM)
    return pl.pallas_call(
        functools.partial(_net_kernel, moments),
        out_shape=jax.ShapeDtypeStruct((moments, h0 - 32, out_w), jnp.bfloat16),
        in_specs=[pl.BlockSpec(memory_space=pltpu.SMEM)] + [vspec] * 9,
        out_specs=vspec,
        scratch_shapes=[
            pltpu.VMEM((h0 - 2, 3 * hid, LANES), jnp.bfloat16),
            pltpu.VMEM((h0 - 6, 3 * hid, LANES), jnp.bfloat16),
        ],
        compiler_params=pltpu.CompilerParams(vmem_limit_bytes=60 * 1024 * 1024),
    )(*args)


def with_halo(cells, sides, width):
    for axis, dim in sides:
        count = lax.axis_size(axis)
        ends = count - 1
        head = lax.slice_in_dim(cells, 0, width, axis=dim)
        tail = lax.slice_in_dim(cells, cells.shape[dim] - width, cells.shape[dim], axis=dim)
        cells = jnp.concatenate(
            [
                lax.ppermute(tail, axis, [(i, (i + 1) % count) for i in range(ends)]),
                cells,
                lax.ppermute(head, axis, [((i + 1) % count, i) for i in range(ends)]),
            ],
            axis=dim,
        )
    return cells


def body(
    state,
    tile_ids,
    kernel_one,
    bias_one,
    kernel_two,
    bias_two,
    kernel_three,
    bias_three,
    kernel_flux,
    bias_flux,
):
    moments, block_h, block_w = state.shape
    col_count = lax.axis_size("col")
    row_count = lax.axis_size("row")
    my_row = lax.axis_index("row")
    my_col = lax.axis_index("col")
    margin = sum(dilations) + 1
    per_row = block_h // TILE
    per_col = block_w // TILE
    per_block = per_row * per_col
    grid_h = block_h * row_count
    grid_w = block_w * col_count
    layers = (
        (kernel_one, bias_one),
        (kernel_two, bias_two),
        (kernel_three, bias_three),
        (kernel_flux, bias_flux),
    )
    listed = tile_ids[0]
    mine = (listed // per_block) == my_col
    local_ids = listed % per_block
    chosen = jnp.any(
        mine[None, :] & (local_ids[None, :] == jnp.arange(per_block, dtype=jnp.int32)[:, None]), axis=1
    )
    own_mask = jnp.broadcast_to(
        chosen.reshape(per_row, 1, per_col, 1), (per_row, TILE, per_col, TILE)
    ).reshape(1, block_h, block_w)
    spare = jnp.zeros((16 - moments - 1, block_h, block_w), state.dtype)
    marked = jnp.concatenate([state, own_mask.astype(state.dtype), spare], axis=0)
    rows_done = jnp.concatenate(
        [
            lax.ppermute(marked[:, -margin:], "row", [(i, i + 1) for i in range(row_count - 1)]),
            marked,
            lax.ppermute(marked[:, :margin], "row", [(i + 1, i) for i in range(row_count - 1)]),
        ],
        axis=1,
    ).transpose(1, 0, 2)
    ext_h = rows_done.shape[0]
    ext_w = block_w + 2 * margin
    ends = col_count - 1
    x = jnp.concatenate(
        [
            lax.ppermute(rows_done[:, :, -margin:], "col", [(i, i + 1) for i in range(ends)]),
            rows_done,
            lax.ppermute(rows_done[:, :, :margin], "col", [(i + 1, i) for i in range(ends)]),
            jnp.zeros((ext_h, 16, LANES - ext_w), state.dtype),
        ],
        axis=2,
    )
    lims = []
    offset = margin
    out_h, out_w = ext_h, ext_w
    for spread in dilations:
        offset = offset - spread
        out_h, out_w = out_h - 2 * spread, out_w - 2 * spread
        top = offset - my_row * block_h
        left = offset - my_col * block_w
        lims += [
            jnp.maximum(top, 0),
            jnp.minimum(out_h, grid_h + top),
            jnp.maximum(left, 0),
            jnp.minimum(out_w, grid_w + left),
        ]
    lims = jnp.stack(lims).astype(jnp.int32)

    closure = run_net(x, lims, layers, block_w, 32)
    return closure


def solution(mesh):
    return jax.shard_map(
        body,
        mesh=mesh,
        in_specs=(P(None, "row", "col"), P("row", None), P(), P(), P(), P(), P(), P(), P(), P()),
        out_specs=P(None, "row", "col"),
        check_vma=False,
    )
```

```python
import functools
import jax
import jax.numpy as jnp
from jax import lax
from jax.experimental import pallas as pl
from jax.experimental.pallas import tpu as pltpu
from jax.sharding import PartitionSpec as P

TILE = 64


dilations = (1, 2, 4, 8)
LANES = 384


def _net_kernel(mark, lim_ref, x_ref, k1, b1, k2, b2, k3, b3, kf, bfl, out_ref, buf_a, buf_b):
    lanes = lax.broadcasted_iota(jnp.int32, (1, LANES), 1)

    def layer(src, dst, n_rows, spread, kmat, bias, index, last):
        kv = kmat[...]
        bv = bias[...]
        if not last:
            after = dilations[index + 1]
            row_lo = lim_ref[4 * index]
            row_hi = lim_ref[4 * index + 1]
            col_ok = (lanes >= lim_ref[4 * index + 2]) & (lanes < lim_ref[4 * index + 3])

        def row(y, carry):
            pieces = []
            for a in range(3):
                line = src[y + spread * a]
                if index == 0:
                    for e in range(3):
                        pieces.append(line if e == 0 else pltpu.roll(line, LANES - spread * e, 1))
                else:
                    pieces.append(line)
            col = jnp.concatenate(pieces, axis=0)
            acc = jnp.dot(kv, col, preferred_element_type=jnp.float32) + bv
            if last:
                reach = sum(dilations)
                flag = x_ref[y + reach].astype(jnp.float32)[mark : mark + 1]
                flag = pltpu.roll(flag, LANES - reach, 1)
                dst[y, : acc.shape[0]] = jnp.where(flag > 0, acc, 0.0).astype(dst.dtype)
            else:
                half = 0.5 * acc
                act = half + half * jnp.tanh(half)
                keep = col_ok & (y >= row_lo) & (y < row_hi)
                kept = jnp.where(keep, act, 0.0).astype(dst.dtype)
                dst[y] = jnp.concatenate(
                    [kept] + [pltpu.roll(kept, LANES - after * e, 1) for e in (1, 2)], axis=0
                )
            return carry

        lax.fori_loop(0, n_rows, row, 0, unroll=(8, 14, 16, 13)[index])

    h0 = x_ref.shape[0] - 2
    h1 = h0 - 2
    h2 = h1 - 4
    h3 = h2 - 8
    h4 = h3 - 16
    layer(x_ref, buf_a, h1 + 2, 1, k1, b1, 0, False)
    layer(buf_a, buf_b, h2, 2, k2, b2, 1, False)
    layer(buf_b, buf_a, h3, 4, k3, b3, 2, False)
    layer(buf_a, buf_b, h4, 8, kf, bfl, 3, True)
    half_ch = kf.shape[0] // 2

    def close_row(y):
        across = buf_b[y + 1, :half_ch].astype(jnp.float32)
        down = buf_b[y + 2, half_ch : 2 * half_ch].astype(jnp.float32) - buf_b[y, half_ch : 2 * half_ch].astype(jnp.float32)
        diff = (pltpu.roll(across, LANES - 2, 1) - across) + pltpu.roll(down, LANES - 1, 1)
        return (-0.5 * diff)[: out_ref.shape[0], : out_ref.shape[2]]

    def close(t, carry):
        y = pl.multiple_of(16 * t, 16)
        group = jnp.stack([close_row(y + k) for k in range(16)], axis=1)
        out_ref[:, pl.ds(y, 16), :] = group.astype(out_ref.dtype)
        return carry

    lax.fori_loop(0, (h4 - 2) // 16, close, 0)


def _kmat(kernel, cin):
    o, c = kernel.shape[:2]
    k = jnp.pad(kernel, ((0, 0), (0, cin - c), (0, 0), (0, 0)))
    return k.transpose(0, 2, 3, 1).reshape(o, 9 * cin)


def run_net(x, lims, layers, out_w, out_ch):
    (k1, b1), (k2, b2), (k3, b3), (kf, bf) = layers
    hid = k1.shape[0]
    h0 = x.shape[0] - 2
    moments = kf.shape[0] // 2
    gap = out_ch // 2 - moments
    kf_p = jnp.concatenate(
        [jnp.pad(part, ((0, gap), (0, 0), (0, 0), (0, 0))) for part in (kf[:moments], kf[moments:])], axis=0
    )
    bf_p = jnp.concatenate([jnp.pad(part, (0, gap)) for part in (bf[:moments], bf[moments:])])
    args = (
        lims, x,
        _kmat(k1, x.shape[1]), b1.reshape(-1, 1),
        _kmat(k2, hid), b2.reshape(-1, 1),
        _kmat(k3, hid), b3.reshape(-1, 1),
        _kmat(kf_p, hid), bf_p.reshape(-1, 1),
    )
    vspec = pl.BlockSpec(memory_space=pltpu.VMEM)
    return pl.pallas_call(
        functools.partial(_net_kernel, moments),
        out_shape=jax.ShapeDtypeStruct((moments, h0 - 32, out_w), jnp.bfloat16),
        in_specs=[pl.BlockSpec(memory_space=pltpu.SMEM)] + [vspec] * 9,
        out_specs=vspec,
        scratch_shapes=[
            pltpu.VMEM((h0, 3 * hid, LANES), jnp.bfloat16),
            pltpu.VMEM((h0 - 6, 3 * hid, LANES), jnp.bfloat16),
        ],
        compiler_params=pltpu.CompilerParams(vmem_limit_bytes=60 * 1024 * 1024),
    )(*args)


def with_halo(cells, sides, width):
    for axis, dim in sides:
        count = lax.axis_size(axis)
        ends = count - 1
        head = lax.slice_in_dim(cells, 0, width, axis=dim)
        tail = lax.slice_in_dim(cells, cells.shape[dim] - width, cells.shape[dim], axis=dim)
        cells = jnp.concatenate(
            [
                lax.ppermute(tail, axis, [(i, (i + 1) % count) for i in range(ends)]),
                cells,
                lax.ppermute(head, axis, [((i + 1) % count, i) for i in range(ends)]),
            ],
            axis=dim,
        )
    return cells


def body(
    state,
    tile_ids,
    kernel_one,
    bias_one,
    kernel_two,
    bias_two,
    kernel_three,
    bias_three,
    kernel_flux,
    bias_flux,
):
    moments, block_h, block_w = state.shape
    col_count = lax.axis_size("col")
    row_count = lax.axis_size("row")
    my_row = lax.axis_index("row")
    my_col = lax.axis_index("col")
    margin = sum(dilations) + 1
    per_row = block_h // TILE
    per_col = block_w // TILE
    per_block = per_row * per_col
    grid_h = block_h * row_count
    grid_w = block_w * col_count
    layers = (
        (kernel_one, bias_one),
        (kernel_two, bias_two),
        (kernel_three, bias_three),
        (kernel_flux, bias_flux),
    )
    listed = tile_ids[0]
    mine = (listed // per_block) == my_col
    local_ids = listed % per_block
    chosen = jnp.any(
        mine[None, :] & (local_ids[None, :] == jnp.arange(per_block, dtype=jnp.int32)[:, None]), axis=1
    )
    own_mask = jnp.broadcast_to(
        chosen.reshape(per_row, 1, per_col, 1), (per_row, TILE, per_col, TILE)
    ).reshape(1, block_h, block_w)
    spare = jnp.zeros((16 - moments - 1, block_h, block_w), state.dtype)
    marked = jnp.concatenate([state, own_mask.astype(state.dtype), spare], axis=0)
    rows_done = jnp.concatenate(
        [
            lax.ppermute(marked[:, -margin:], "row", [(i, i + 1) for i in range(row_count - 1)]),
            marked,
            lax.ppermute(marked[:, :margin], "row", [(i + 1, i) for i in range(row_count - 1)]),
        ],
        axis=1,
    ).transpose(1, 0, 2)
    ext_h = rows_done.shape[0]
    ext_w = block_w + 2 * margin
    ends = col_count - 1
    x = jnp.concatenate(
        [
            lax.ppermute(rows_done[:, :, -margin:], "col", [(i, i + 1) for i in range(ends)]),
            rows_done,
            lax.ppermute(rows_done[:, :, :margin], "col", [(i + 1, i) for i in range(ends)]),
            jnp.zeros((ext_h, 16, LANES - ext_w), state.dtype),
        ],
        axis=2,
    )
    x = jnp.concatenate([x, jnp.zeros((2,) + x.shape[1:], x.dtype)], axis=0)
    lims = []
    offset = margin
    out_h, out_w = ext_h, ext_w
    for spread in dilations:
        offset = offset - spread
        out_h, out_w = out_h - 2 * spread, out_w - 2 * spread
        top = offset - my_row * block_h
        left = offset - my_col * block_w
        lims += [
            jnp.maximum(top, 0),
            jnp.minimum(out_h, grid_h + top),
            jnp.maximum(left, 0),
            jnp.minimum(out_w, grid_w + left),
        ]
    lims = jnp.stack(lims).astype(jnp.int32)

    closure = run_net(x, lims, layers, block_w, 32)
    return closure


def solution(mesh):
    return jax.shard_map(
        body,
        mesh=mesh,
        in_specs=(P(None, "row", "col"), P("row", None), P(), P(), P(), P(), P(), P(), P(), P()),
        out_specs=P(None, "row", "col"),
        check_vma=False,
    )
```

```python
import functools
import jax
import jax.numpy as jnp
from jax import lax
from jax.experimental import pallas as pl
from jax.experimental.pallas import tpu as pltpu
from jax.sharding import PartitionSpec as P

TILE = 64


dilations = (1, 2, 4, 8)
LANES = 384


def _net_kernel(mark, lim_ref, x_ref, k1, b1, k2, b2, k3, b3, kf, bfl, out_ref, buf_a, buf_b):
    lanes = lax.broadcasted_iota(jnp.int32, (1, LANES), 1)

    def layer(src, dst, n_rows, spread, kmat, bias, index, last):
        kv = kmat[...]
        bv = bias[...]
        if not last:
            after = dilations[index + 1]
            row_lo = lim_ref[4 * index]
            row_hi = lim_ref[4 * index + 1]
            col_ok = (lanes >= lim_ref[4 * index + 2]) & (lanes < lim_ref[4 * index + 3])

        def row(y, carry):
            pieces = []
            for a in range(3):
                line = src[y + spread * a]
                if index == 0:
                    for e in range(3):
                        pieces.append(line if e == 0 else pltpu.roll(line, LANES - spread * e, 1))
                else:
                    pieces.append(line)
            col = jnp.concatenate(pieces, axis=0)
            acc = jnp.dot(kv, col, preferred_element_type=jnp.float32) + bv
            if last:
                reach = sum(dilations)
                flag = x_ref[y + reach].astype(jnp.float32)[mark : mark + 1]
                flag = pltpu.roll(flag, LANES - reach, 1)
                dst[y, : acc.shape[0]] = jnp.where(flag > 0, acc, 0.0).astype(dst.dtype)
            else:
                half = 0.5 * acc
                act = half + half * jnp.tanh(half)
                keep = col_ok & (y >= row_lo) & (y < row_hi)
                kept = jnp.where(keep, act, 0.0).astype(dst.dtype)
                dst[y] = jnp.concatenate(
                    [kept] + [pltpu.roll(kept, LANES - after * e, 1) for e in (1, 2)], axis=0
                )
            return carry

        lax.fori_loop(0, n_rows, row, 0, unroll=(8, 22, 16, 13)[index])

    h0 = x_ref.shape[0] - 2
    h1 = h0 - 2
    h2 = h1 - 4
    h3 = h2 - 8
    h4 = h3 - 16
    layer(x_ref, buf_a, h1 + 2, 1, k1, b1, 0, False)
    layer(buf_a, buf_b, h2, 2, k2, b2, 1, False)
    layer(buf_b, buf_a, h3, 4, k3, b3, 2, False)
    layer(buf_a, buf_b, h4, 8, kf, bfl, 3, True)
    half_ch = kf.shape[0] // 2

    def close_row(y):
        across = buf_b[y + 1, :half_ch].astype(jnp.float32)
        down = buf_b[y + 2, half_ch : 2 * half_ch].astype(jnp.float32) - buf_b[y, half_ch : 2 * half_ch].astype(jnp.float32)
        diff = (pltpu.roll(across, LANES - 2, 1) - across) + pltpu.roll(down, LANES - 1, 1)
        return (-0.5 * diff)[: out_ref.shape[0], : out_ref.shape[2]]

    def close(t, carry):
        y = pl.multiple_of(16 * t, 16)
        group = jnp.stack([close_row(y + k) for k in range(16)], axis=1)
        out_ref[:, pl.ds(y, 16), :] = group.astype(out_ref.dtype)
        return carry

    lax.fori_loop(0, (h4 - 2) // 16, close, 0)


def _kmat(kernel, cin):
    o, c = kernel.shape[:2]
    k = jnp.pad(kernel, ((0, 0), (0, cin - c), (0, 0), (0, 0)))
    return k.transpose(0, 2, 3, 1).reshape(o, 9 * cin)


def run_net(x, lims, layers, out_w, out_ch):
    (k1, b1), (k2, b2), (k3, b3), (kf, bf) = layers
    hid = k1.shape[0]
    h0 = x.shape[0] - 2
    moments = kf.shape[0] // 2
    gap = out_ch // 2 - moments
    kf_p = jnp.concatenate(
        [jnp.pad(part, ((0, gap), (0, 0), (0, 0), (0, 0))) for part in (kf[:moments], kf[moments:])], axis=0
    )
    bf_p = jnp.concatenate([jnp.pad(part, (0, gap)) for part in (bf[:moments], bf[moments:])])
    args = (
        lims, x,
        _kmat(k1, x.shape[1]), b1.reshape(-1, 1),
        _kmat(k2, hid), b2.reshape(-1, 1),
        _kmat(k3, hid), b3.reshape(-1, 1),
        _kmat(kf_p, hid), bf_p.reshape(-1, 1),
    )
    vspec = pl.BlockSpec(memory_space=pltpu.VMEM)
    return pl.pallas_call(
        functools.partial(_net_kernel, moments),
        out_shape=jax.ShapeDtypeStruct((moments, h0 - 32, out_w), jnp.bfloat16),
        in_specs=[pl.BlockSpec(memory_space=pltpu.SMEM)] + [vspec] * 9,
        out_specs=vspec,
        scratch_shapes=[
            pltpu.VMEM((h0, 3 * hid, LANES), jnp.bfloat16),
            pltpu.VMEM((h0 - 6, 3 * hid, LANES), jnp.bfloat16),
        ],
        compiler_params=pltpu.CompilerParams(vmem_limit_bytes=60 * 1024 * 1024),
    )(*args)


def with_halo(cells, sides, width):
    for axis, dim in sides:
        count = lax.axis_size(axis)
        ends = count - 1
        head = lax.slice_in_dim(cells, 0, width, axis=dim)
        tail = lax.slice_in_dim(cells, cells.shape[dim] - width, cells.shape[dim], axis=dim)
        cells = jnp.concatenate(
            [
                lax.ppermute(tail, axis, [(i, (i + 1) % count) for i in range(ends)]),
                cells,
                lax.ppermute(head, axis, [((i + 1) % count, i) for i in range(ends)]),
            ],
            axis=dim,
        )
    return cells


def body(
    state,
    tile_ids,
    kernel_one,
    bias_one,
    kernel_two,
    bias_two,
    kernel_three,
    bias_three,
    kernel_flux,
    bias_flux,
):
    moments, block_h, block_w = state.shape
    col_count = lax.axis_size("col")
    row_count = lax.axis_size("row")
    my_row = lax.axis_index("row")
    my_col = lax.axis_index("col")
    margin = sum(dilations) + 1
    per_row = block_h // TILE
    per_col = block_w // TILE
    per_block = per_row * per_col
    grid_h = block_h * row_count
    grid_w = block_w * col_count
    layers = (
        (kernel_one, bias_one),
        (kernel_two, bias_two),
        (kernel_three, bias_three),
        (kernel_flux, bias_flux),
    )
    listed = tile_ids[0]
    mine = (listed // per_block) == my_col
    local_ids = listed % per_block
    chosen = jnp.any(
        mine[None, :] & (local_ids[None, :] == jnp.arange(per_block, dtype=jnp.int32)[:, None]), axis=1
    )
    own_mask = jnp.broadcast_to(
        chosen.reshape(per_row, 1, per_col, 1), (per_row, TILE, per_col, TILE)
    ).reshape(1, block_h, block_w)
    spare = jnp.zeros((16 - moments - 1, block_h, block_w), state.dtype)
    marked = jnp.concatenate([state, own_mask.astype(state.dtype), spare], axis=0)
    rows_done = jnp.concatenate(
        [
            lax.ppermute(marked[:, -margin:], "row", [(i, i + 1) for i in range(row_count - 1)]),
            marked,
            lax.ppermute(marked[:, :margin], "row", [(i + 1, i) for i in range(row_count - 1)]),
        ],
        axis=1,
    ).transpose(1, 0, 2)
    ext_h = rows_done.shape[0]
    ext_w = block_w + 2 * margin
    ends = col_count - 1
    x = jnp.concatenate(
        [
            lax.ppermute(rows_done[:, :, -margin:], "col", [(i, i + 1) for i in range(ends)]),
            rows_done,
            lax.ppermute(rows_done[:, :, :margin], "col", [(i + 1, i) for i in range(ends)]),
            jnp.zeros((ext_h, 16, LANES - ext_w), state.dtype),
        ],
        axis=2,
    )
    x = jnp.concatenate([x, jnp.zeros((2,) + x.shape[1:], x.dtype)], axis=0)
    lims = []
    offset = margin
    out_h, out_w = ext_h, ext_w
    for spread in dilations:
        offset = offset - spread
        out_h, out_w = out_h - 2 * spread, out_w - 2 * spread
        top = offset - my_row * block_h
        left = offset - my_col * block_w
        lims += [
            jnp.maximum(top, 0),
            jnp.minimum(out_h, grid_h + top),
            jnp.maximum(left, 0),
            jnp.minimum(out_w, grid_w + left),
        ]
    lims = jnp.stack(lims).astype(jnp.int32)

    closure = run_net(x, lims, layers, block_w, 32)
    return closure


def solution(mesh):
    return jax.shard_map(
        body,
        mesh=mesh,
        in_specs=(P(None, "row", "col"), P("row", None), P(), P(), P(), P(), P(), P(), P(), P()),
        out_specs=P(None, "row", "col"),
        check_vma=False,
    )
```

```python
import functools
import jax
import jax.numpy as jnp
from jax import lax
from jax.experimental import pallas as pl
from jax.experimental.pallas import tpu as pltpu
from jax.sharding import PartitionSpec as P

TILE = 64


dilations = (1, 2, 4, 8)
LANES = 384


def _net_kernel(mark, lim_ref, x_ref, k1, b1, k2, b2, k3, b3, kf, bfl, out_ref, buf_a, buf_b):
    lanes = lax.broadcasted_iota(jnp.int32, (1, LANES), 1)

    def layer(src, dst, n_rows, spread, kmat, bias, index, last):
        kv = kmat[...]
        bv = bias[...]
        if not last:
            after = dilations[index + 1]
            row_lo = lim_ref[4 * index]
            row_hi = lim_ref[4 * index + 1]
            col_ok = (lanes >= lim_ref[4 * index + 2]) & (lanes < lim_ref[4 * index + 3])

        def row(y, carry):
            pieces = []
            for a in range(3):
                line = src[y + spread * a]
                if index == 0:
                    for e in range(3):
                        pieces.append(line if e == 0 else pltpu.roll(line, LANES - spread * e, 1))
                else:
                    pieces.append(line)
            col = jnp.concatenate(pieces, axis=0)
            acc = jnp.dot(kv, col, preferred_element_type=jnp.float32) + bv
            if last:
                reach = sum(dilations)
                flag = x_ref[y + reach].astype(jnp.float32)[mark : mark + 1]
                flag = pltpu.roll(flag, LANES - reach, 1)
                dst[y, : acc.shape[0]] = jnp.where(flag > 0, acc, 0.0).astype(dst.dtype)
            else:
                half = 0.5 * acc
                act = half + half * jnp.tanh(half)
                keep = col_ok & (y >= row_lo) & (y < row_hi)
                kept = jnp.where(keep, act, 0.0).astype(dst.dtype)
                dst[y] = jnp.concatenate(
                    [kept] + [pltpu.roll(kept, LANES - after * e, 1) for e in (1, 2)], axis=0
                )
            return carry

        lax.fori_loop(0, n_rows, row, 0, unroll=(8, 22, 16, 26)[index])

    h0 = x_ref.shape[0] - 2
    h1 = h0 - 2
    h2 = h1 - 4
    h3 = h2 - 8
    h4 = h3 - 16
    layer(x_ref, buf_a, h1 + 2, 1, k1, b1, 0, False)
    layer(buf_a, buf_b, h2, 2, k2, b2, 1, False)
    layer(buf_b, buf_a, h3, 4, k3, b3, 2, False)
    layer(buf_a, buf_b, h4, 8, kf, bfl, 3, True)
    half_ch = kf.shape[0] // 2

    def close_row(y):
        across = buf_b[y + 1, :half_ch].astype(jnp.float32)
        down = buf_b[y + 2, half_ch : 2 * half_ch].astype(jnp.float32) - buf_b[y, half_ch : 2 * half_ch].astype(jnp.float32)
        diff = (pltpu.roll(across, LANES - 2, 1) - across) + pltpu.roll(down, LANES - 1, 1)
        return (-0.5 * diff)[: out_ref.shape[0], : out_ref.shape[2]]

    def close(t, carry):
        y = pl.multiple_of(16 * t, 16)
        group = jnp.stack([close_row(y + k) for k in range(16)], axis=1)
        out_ref[:, pl.ds(y, 16), :] = group.astype(out_ref.dtype)
        return carry

    lax.fori_loop(0, (h4 - 2) // 16, close, 0)


def _kmat(kernel, cin):
    o, c = kernel.shape[:2]
    k = jnp.pad(kernel, ((0, 0), (0, cin - c), (0, 0), (0, 0)))
    return k.transpose(0, 2, 3, 1).reshape(o, 9 * cin)


def run_net(x, lims, layers, out_w, out_ch):
    (k1, b1), (k2, b2), (k3, b3), (kf, bf) = layers
    hid = k1.shape[0]
    h0 = x.shape[0] - 2
    moments = kf.shape[0] // 2
    gap = out_ch // 2 - moments
    kf_p = jnp.concatenate(
        [jnp.pad(part, ((0, gap), (0, 0), (0, 0), (0, 0))) for part in (kf[:moments], kf[moments:])], axis=0
    )
    bf_p = jnp.concatenate([jnp.pad(part, (0, gap)) for part in (bf[:moments], bf[moments:])])
    args = (
        lims, x,
        _kmat(k1, x.shape[1]), b1.reshape(-1, 1),
        _kmat(k2, hid), b2.reshape(-1, 1),
        _kmat(k3, hid), b3.reshape(-1, 1),
        _kmat(kf_p, hid), bf_p.reshape(-1, 1),
    )
    vspec = pl.BlockSpec(memory_space=pltpu.VMEM)
    return pl.pallas_call(
        functools.partial(_net_kernel, moments),
        out_shape=jax.ShapeDtypeStruct((moments, h0 - 32, out_w), jnp.bfloat16),
        in_specs=[pl.BlockSpec(memory_space=pltpu.SMEM)] + [vspec] * 9,
        out_specs=vspec,
        scratch_shapes=[
            pltpu.VMEM((h0, 3 * hid, LANES), jnp.bfloat16),
            pltpu.VMEM((h0 - 6, 3 * hid, LANES), jnp.bfloat16),
        ],
        compiler_params=pltpu.CompilerParams(vmem_limit_bytes=60 * 1024 * 1024),
    )(*args)


def with_halo(cells, sides, width):
    for axis, dim in sides:
        count = lax.axis_size(axis)
        ends = count - 1
        head = lax.slice_in_dim(cells, 0, width, axis=dim)
        tail = lax.slice_in_dim(cells, cells.shape[dim] - width, cells.shape[dim], axis=dim)
        cells = jnp.concatenate(
            [
                lax.ppermute(tail, axis, [(i, (i + 1) % count) for i in range(ends)]),
                cells,
                lax.ppermute(head, axis, [((i + 1) % count, i) for i in range(ends)]),
            ],
            axis=dim,
        )
    return cells


def body(
    state,
    tile_ids,
    kernel_one,
    bias_one,
    kernel_two,
    bias_two,
    kernel_three,
    bias_three,
    kernel_flux,
    bias_flux,
):
    moments, block_h, block_w = state.shape
    col_count = lax.axis_size("col")
    row_count = lax.axis_size("row")
    my_row = lax.axis_index("row")
    my_col = lax.axis_index("col")
    margin = sum(dilations) + 1
    per_row = block_h // TILE
    per_col = block_w // TILE
    per_block = per_row * per_col
    grid_h = block_h * row_count
    grid_w = block_w * col_count
    layers = (
        (kernel_one, bias_one),
        (kernel_two, bias_two),
        (kernel_three, bias_three),
        (kernel_flux, bias_flux),
    )
    listed = tile_ids[0]
    mine = (listed // per_block) == my_col
    local_ids = listed % per_block
    chosen = jnp.any(
        mine[None, :] & (local_ids[None, :] == jnp.arange(per_block, dtype=jnp.int32)[:, None]), axis=1
    )
    own_mask = jnp.broadcast_to(
        chosen.reshape(per_row, 1, per_col, 1), (per_row, TILE, per_col, TILE)
    ).reshape(1, block_h, block_w)
    spare = jnp.zeros((16 - moments - 1, block_h, block_w), state.dtype)
    marked = jnp.concatenate([state, own_mask.astype(state.dtype), spare], axis=0)
    rows_done = jnp.concatenate(
        [
            lax.ppermute(marked[:, -margin:], "row", [(i, i + 1) for i in range(row_count - 1)]),
            marked,
            lax.ppermute(marked[:, :margin], "row", [(i + 1, i) for i in range(row_count - 1)]),
        ],
        axis=1,
    ).transpose(1, 0, 2)
    ext_h = rows_done.shape[0]
    ext_w = block_w + 2 * margin
    ends = col_count - 1
    x = jnp.concatenate(
        [
            lax.ppermute(rows_done[:, :, -margin:], "col", [(i, i + 1) for i in range(ends)]),
            rows_done,
            lax.ppermute(rows_done[:, :, :margin], "col", [(i + 1, i) for i in range(ends)]),
            jnp.zeros((ext_h, 16, LANES - ext_w), state.dtype),
        ],
        axis=2,
    )
    x = jnp.concatenate([x, jnp.zeros((2,) + x.shape[1:], x.dtype)], axis=0)
    lims = []
    offset = margin
    out_h, out_w = ext_h, ext_w
    for spread in dilations:
        offset = offset - spread
        out_h, out_w = out_h - 2 * spread, out_w - 2 * spread
        top = offset - my_row * block_h
        left = offset - my_col * block_w
        lims += [
            jnp.maximum(top, 0),
            jnp.minimum(out_h, grid_h + top),
            jnp.maximum(left, 0),
            jnp.minimum(out_w, grid_w + left),
        ]
    lims = jnp.stack(lims).astype(jnp.int32)

    closure = run_net(x, lims, layers, block_w, 32)
    return closure


def solution(mesh):
    return jax.shard_map(
        body,
        mesh=mesh,
        in_specs=(P(None, "row", "col"), P("row", None), P(), P(), P(), P(), P(), P(), P(), P()),
        out_specs=P(None, "row", "col"),
        check_vma=False,
    )
```
